128 devices in a mesh: row: 8 (over z, core), col: 16 (over x, y).
Axes of the slice: x: 4, y: 4, z: 4, core: 2. Of those that a mesh axis runs over, the one named last changes fastest.
Arguments:
- image: bfloat16 [128, 512, 768], P('row', 'col'), may hold values from -6 to 6
- dw_kernel: float32 [768, 49], replicated, may hold values from -0.875 to 0.875
- ln_gain: float32 [768], replicated, may hold values from 0.25 to 1.75
- w_in: bfloat16 [768, 3072], P('col'), may hold values from -0.21875 to 0.21875
- b_in: float32 [3072], replicated, may hold values from -3 to 3
- w_out: bfloat16 [3072, 768], P('col'), may hold values from -0.109375 to 0.109375
- layer_scale: float32 [768], replicated, may hold values from 0.5 to 1.5
- cotangent: bfloat16 [128, 512, 768], P('row', 'col'), may hold values from -8 to 8
Outputs:
- out_map: bfloat16 [128, 512, 768], P('row', 'col')
- grad_image: bfloat16 [128, 512, 768], P('row', 'col')
- grad_kernel: float32 [768, 49], P(('row', 'col'))
- grad_w_in: float32 [768, 3072], P('col')
- grad_w_out: float32 [3072, 768], P('col')
- grad_b_in: float32 [3072], replicated
- grad_gain: float32 [768], replicated
- grad_scale: float32 [768], replicated
The draws below stay inside these ranges and needn't reach their ends.
All inputs are finite; a program needn't handle non-finite values.
Results may differ from the reference program's by a relative error of at most 0.0071.
Values may be sent and summed in bfloat16 or wider, within the bound.
No kernel may reach another device: no remote copies, remote signals or barrier semaphores. Data moves between devices by JAX's collectives and lax.ppermute only.
A program may use at most 128 MiB of HBM per device.

```python
import math
import jax
import jax.numpy as jnp
from jax import lax

D = 768
FF = 3072
KSIZE = 7
DILATE = 2
REACH = 6
MAP_ROWS = 128
MAP_COLS = 512


def draw_cotangent(key, part):
    row_place = jnp.arange(MAP_ROWS, dtype=jnp.float32)[:, None, None] / MAP_ROWS
    col_place = jnp.arange(MAP_COLS, dtype=jnp.float32)[None, :, None] / MAP_COLS
    ramp = 0.5 + row_place + 0.5 * col_place
    base = jax.random.truncated_normal(key, -4.0, 4.0, (MAP_ROWS, MAP_COLS, D), jnp.float32)
    return (base * ramp).astype(jnp.bfloat16)


def steps_of(own_key, shape, cuts, smallest, top_value):
    factor_of, own = 1.0, jax.random.fold_in(own_key, 6)
    for dim, blocks in cuts:
        draws = jnp.exp(jax.random.uniform(jax.random.fold_in(own, dim), (blocks,), jnp.float32, smallest / len(cuts), top_value / len(cuts)))
        factor_of = factor_of * jnp.repeat(draws, shape[dim] // blocks).reshape([-1 if axis == dim else 1 for axis in range(len(shape))])
    return factor_of


def noise(rng, shape, spread, bound, split=(), kind=jnp.bfloat16):
    level = steps_of(rng, shape, split, -0.22, 0.18) if split else 1.0
    result = jax.random.normal(rng, shape, jnp.float32) * spread * level
    return jnp.minimum(jnp.maximum(result, -bound), bound).astype(kind)


def setup_inputs(seed: int = 0) -> dict:
    keys = jax.random.split(jax.random.key(seed), 9)
    image = noise(keys[0], (MAP_ROWS, MAP_COLS, D), 1.0, 6.0, ((0, 8), (1, 16)))
    dw_kernel = noise(keys[1], (D, KSIZE * KSIZE), (KSIZE * KSIZE) ** -0.5, 0.875, (), jnp.float32)
    ln_gain = jnp.clip(1.0 + 0.15 * jax.random.normal(keys[2], (D,), jnp.float32), 0.25, 1.75)
    w_in = noise(keys[3], (D, FF), D ** -0.5, 0.21875, ((0, 16),))
    b_in = noise(keys[4], (FF,), 0.5, 3.0, (), jnp.float32)
    w_out = noise(keys[5], (FF, D), FF ** -0.5, 0.109375, ((0, 16),))
    layer_scale = jnp.clip(jax.random.uniform(keys[6], (D,), jnp.float32, 0.5, 1.5), 0.5, 1.5)
    cotangent = draw_cotangent(jax.random.fold_in(keys[8], 71), 0)
    return dict(image=image, dw_kernel=dw_kernel, ln_gain=ln_gain, w_in=w_in, b_in=b_in, w_out=w_out, layer_scale=layer_scale, cotangent=cotangent)


EPSILON = 1e-06

def normal_cdf(values):
    return 0.5 * (1.0 + jax.scipy.special.erf(values * 0.7071067811865476))

def gelu_exact(values):
    return values * normal_cdf(values)

def gelu_slope(values):
    return normal_cdf(values) + values * jnp.exp(-0.5 * values * values) * 0.3989422804014327

def spatial_stencil(padded, tap_table, height, breadth):
    summed = jnp.zeros((height, breadth, tap_table.shape[0]), jnp.float32)
    for tap_row in range(KSIZE):
        for tap_col in range(KSIZE):
            window = padded[DILATE * tap_row:DILATE * tap_row + height, DILATE * tap_col:DILATE * tap_col + breadth, :].astype(jnp.float32)
            summed = summed + tap_table[:, KSIZE * tap_row + tap_col] * window
    return summed

def spatial_taps(padded, gradient, height, breadth):
    columns = []
    for tap_row in range(KSIZE):
        for tap_col in range(KSIZE):
            window = padded[DILATE * tap_row:DILATE * tap_row + height, DILATE * tap_col:DILATE * tap_col + breadth, :].astype(jnp.float32)
            columns.append(lax.optimization_barrier(jnp.sum(gradient * window, axis=(0, 1))))
    return jnp.stack(columns, axis=1)

def reference(image, dw_kernel, ln_gain, w_in, b_in, w_out, layer_scale, cotangent):
    height, breadth, channels = image.shape
    hidden_units = w_in.shape[1]
    pixels = height * breadth
    scale_factor = 1.0 / math.sqrt(pixels)
    padded = jnp.pad(image, ((REACH, REACH), (REACH, REACH), (0, 0)))
    conv_map = spatial_stencil(padded, dw_kernel, height, breadth).astype(jnp.bfloat16)
    conv_rows = conv_map.astype(jnp.float32).reshape(pixels, channels)
    average = lax.optimization_barrier(jnp.mean(conv_rows, axis=1, keepdims=True))
    centered = conv_rows - average
    inverse = lax.rsqrt(lax.optimization_barrier(jnp.mean(centered * centered, axis=1, keepdims=True)) + EPSILON)
    standard = centered * inverse
    normed = (standard * ln_gain).astype(jnp.bfloat16)
    block = math.gcd(pixels, 4096)

    def block_step(carry, pieces):
        sum_in, sum_out, sum_bias, sum_scale = carry
        normed_block, upstream_block, image_block = pieces
        preact = jnp.dot(normed_block, w_in, preferred_element_type=jnp.float32) + b_in
        hidden = gelu_exact(preact).astype(jnp.bfloat16)
        mixed = jnp.dot(hidden, w_out, preferred_element_type=jnp.float32)
        out_block = (image_block.astype(jnp.float32) + layer_scale * mixed).astype(jnp.bfloat16)
        upstream = upstream_block.astype(jnp.float32)
        sum_scale = sum_scale + lax.optimization_barrier(jnp.sum(upstream * mixed, axis=0))
        grad_mix = (upstream * layer_scale).astype(jnp.bfloat16)
        sum_out = sum_out + jnp.dot(hidden.T, grad_mix, preferred_element_type=jnp.float32)
        grad_hidden = jnp.dot(grad_mix, w_out.T, preferred_element_type=jnp.float32)
        grad_pre = grad_hidden * gelu_slope(preact)
        sum_bias = sum_bias + lax.optimization_barrier(jnp.sum(grad_pre, axis=0))
        grad_pre_rounded = grad_pre.astype(jnp.bfloat16)
        sum_in = sum_in + jnp.dot(normed_block.T, grad_pre_rounded, preferred_element_type=jnp.float32)
        grad_norm = jnp.dot(grad_pre_rounded, w_in.T, preferred_element_type=jnp.float32)
        return ((sum_in, sum_out, sum_bias, sum_scale), (out_block, grad_norm))
    initial = (jnp.zeros((channels, hidden_units), jnp.float32), jnp.zeros((hidden_units, channels), jnp.float32), jnp.zeros((hidden_units,), jnp.float32), jnp.zeros((channels,), jnp.float32))
    stacked = (normed.reshape(-1, block, channels), cotangent.reshape(-1, block, channels), image.reshape(-1, block, channels))
    totals, (out_rows, grad_norm) = lax.scan(block_step, initial, stacked)
    sum_in, sum_out, sum_bias, sum_scale = totals
    out_map = out_rows.reshape(height, breadth, channels)
    grad_norm = grad_norm.reshape(pixels, channels)
    grad_gain = lax.optimization_barrier(jnp.sum(grad_norm * standard, axis=0)) * scale_factor
    scaled = grad_norm * ln_gain
    grad_conv = ((scaled - lax.optimization_barrier(jnp.mean(scaled, axis=1, keepdims=True)) - standard * lax.optimization_barrier(jnp.mean(scaled * standard, axis=1, keepdims=True))) * inverse).astype(jnp.bfloat16)
    grad_conv = grad_conv.reshape(height, breadth, channels)
    flipped = dw_kernel.reshape(channels, KSIZE, KSIZE)[:, ::-1, ::-1].reshape(channels, KSIZE * KSIZE)
    grad_pad = jnp.pad(grad_conv, ((REACH, REACH), (REACH, REACH), (0, 0)))
    grad_back = spatial_stencil(grad_pad, flipped, height, breadth).astype(jnp.bfloat16)
    grad_image = (cotangent.astype(jnp.float32) + grad_back.astype(jnp.float32)).astype(jnp.bfloat16)
    grad_kernel = spatial_taps(padded, grad_conv.astype(jnp.float32), height, breadth) * scale_factor
    return (out_map, grad_image, grad_kernel, sum_in * scale_factor, sum_out * scale_factor, sum_bias * scale_factor, grad_gain, sum_scale * scale_factor)
```

```python
import math

import jax
import jax.numpy as jnp
from jax import lax
from jax.sharding import PartitionSpec as P

KSIZE = 7
DILATE = 2
REACH = 6


EPSILON = 1e-06
CONTRACT_ROWS = (((0,), (0,)), ((), ()))
CONTRACT_COLS = (((1,), (1,)), ((), ()))


def normal_cdf(values):
    return 0.5 * (1.0 + jax.scipy.special.erf(values * 0.7071067811865476))


def gelu_exact(values):
    return values * normal_cdf(values)


def gelu_slope(values):
    return normal_cdf(values) + values * jnp.exp(-0.5 * values * values) * 0.3989422804014327


def shift_pairs(count, step):
    if step > 0:
        return [(i, i + 1) for i in range(count - 1)]
    return [(i + 1, i) for i in range(count - 1)]


def add_halo(field):
    row_count = lax.axis_size("row")
    col_count = lax.axis_size("col")
    left = lax.ppermute(field[:, -REACH:, :], "col", shift_pairs(col_count, 1))
    right = lax.ppermute(field[:, :REACH, :], "col", shift_pairs(col_count, -1))
    wide = jnp.concatenate([left, field, right], axis=1)
    top = lax.ppermute(wide[-REACH:], "row", shift_pairs(row_count, 1))
    bottom = lax.ppermute(wide[:REACH], "row", shift_pairs(row_count, -1))
    return jnp.concatenate([top, wide, bottom], axis=0)


def tile_stencil(padded, tap_table, height, breadth):
    summed = jnp.zeros((height, breadth, tap_table.shape[0]), jnp.float32)
    for tap_row in range(KSIZE):
        for tap_col in range(KSIZE):
            window = padded[
                DILATE * tap_row : DILATE * tap_row + height,
                DILATE * tap_col : DILATE * tap_col + breadth,
                :,
            ].astype(jnp.float32)
            summed = summed + tap_table[:, KSIZE * tap_row + tap_col] * window
    return summed


def tile_taps(padded, gradient, height, breadth):
    columns = []
    for tap_row in range(KSIZE):
        for tap_col in range(KSIZE):
            window = padded[
                DILATE * tap_row : DILATE * tap_row + height,
                DILATE * tap_col : DILATE * tap_col + breadth,
                :,
            ].astype(jnp.float32)
            columns.append(jnp.sum(gradient * window, axis=(0, 1)))
    return jnp.stack(columns, axis=1)


def local(image, dw_kernel, ln_gain, w_in, b_in, w_out, layer_scale, cotangent):
    tile_rows, tile_cols, channels = image.shape
    row_count = lax.axis_size("row")
    col_count = lax.axis_size("col")
    group_count = row_count * col_count
    group_size = channels // group_count
    pixels = tile_rows * tile_cols
    scale_factor = 1.0 / math.sqrt(pixels * group_count)
    full_in, full_out = (
        lax.all_gather(w_in, "col", axis=0, tiled=True),
        lax.all_gather(w_out, "col", axis=0, tiled=True),
    )
    flipped = dw_kernel.reshape(channels, KSIZE, KSIZE)[:, ::-1, ::-1].reshape(
        channels, KSIZE * KSIZE
    )
    group_index = lax.axis_index("row") * col_count + lax.axis_index("col")
    padded = add_halo(image)
    conv_tile = tile_stencil(padded, dw_kernel, tile_rows, tile_cols).astype(jnp.bfloat16)
    conv_rows = conv_tile.astype(jnp.float32).reshape(pixels, channels)
    average = jnp.mean(conv_rows, axis=1, keepdims=True)
    centered = conv_rows - average
    inverse = lax.rsqrt(jnp.mean(centered * centered, axis=1, keepdims=True) + EPSILON)
    standard = centered * inverse
    normed = (standard * ln_gain).astype(jnp.bfloat16)
    preact = jnp.dot(normed, full_in, preferred_element_type=jnp.float32) + b_in
    hidden = gelu_exact(preact).astype(jnp.bfloat16)
    mixed = jnp.dot(hidden, full_out, preferred_element_type=jnp.float32)
    out_map = (image.reshape(pixels, channels).astype(jnp.float32) + layer_scale * mixed).astype(
        jnp.bfloat16
    )
    out_map = out_map.reshape(tile_rows, tile_cols, channels)
    upstream = cotangent.reshape(pixels, channels).astype(jnp.float32)
    scale_part = jnp.sum(upstream * mixed, axis=0)
    grad_mix = (upstream * layer_scale).astype(jnp.bfloat16)
    grad_hidden = lax.dot_general(
        grad_mix, full_out, CONTRACT_COLS, preferred_element_type=jnp.float32
    )
    grad_pre = grad_hidden * gelu_slope(preact)
    bias_part = jnp.sum(grad_pre, axis=0)
    grad_pre_rounded = grad_pre.astype(jnp.bfloat16)
    grad_norm = lax.dot_general(
        grad_pre_rounded, full_in, CONTRACT_COLS, preferred_element_type=jnp.float32
    )
    part_in = lax.psum_scatter(
        lax.dot_general(
            normed, grad_pre_rounded, CONTRACT_ROWS, preferred_element_type=jnp.float32
        ),
        "col",
        scatter_dimension=0,
        tiled=True,
    )
    part_out = lax.psum_scatter(
        lax.dot_general(hidden, grad_mix, CONTRACT_ROWS, preferred_element_type=jnp.float32),
        "col",
        scatter_dimension=0,
        tiled=True,
    )
    summed_in, summed_out = lax.psum((part_in, part_out), "row")
    gain_part = jnp.sum(grad_norm * standard, axis=0)
    scaled = grad_norm * ln_gain
    grad_conv = (
        (
            scaled
            - jnp.mean(scaled, axis=1, keepdims=True)
            - standard * jnp.mean(scaled * standard, axis=1, keepdims=True)
        )
        * inverse
    ).astype(jnp.bfloat16)
    grad_conv = grad_conv.reshape(tile_rows, tile_cols, channels)
    grad_padded = add_halo(grad_conv)
    grad_back = tile_stencil(grad_padded, flipped, tile_rows, tile_cols).astype(jnp.bfloat16)
    kernel_part = tile_taps(padded, grad_conv.astype(jnp.float32), tile_rows, tile_cols)
    grad_image = (cotangent.astype(jnp.float32) + grad_back.astype(jnp.float32)).astype(
        jnp.bfloat16
    )
    scale_sum, bias_sum, gain_sum, kernel_sum = lax.psum(
        (scale_part, bias_part, gain_part, kernel_part), ("row", "col")
    )
    grad_kernel = (
        lax.dynamic_slice_in_dim(kernel_sum, group_index * group_size, group_size, 0)
        * scale_factor
    )
    return (
        out_map,
        grad_image,
        grad_kernel,
        summed_in * scale_factor,
        summed_out * scale_factor,
        bias_sum * scale_factor,
        gain_sum * scale_factor,
        scale_sum * scale_factor,
    )


def solution(mesh):
    in_specs = (
        P("row", "col", None),
        P(),
        P(),
        P("col", None),
        P(),
        P("col", None),
        P(),
        P("row", "col", None),
    )
    out_specs = (
        P("row", "col", None),
        P("row", "col", None),
        P(("row", "col"), None),
        P("col", None),
        P("col", None),
        P(),
        P(),
        P(),
    )
    return jax.shard_map(local, mesh=mesh, in_specs=in_specs, out_specs=out_specs, check_vma=False)
```

```python
import math

import jax
import jax.numpy as jnp
from jax import lax
from jax.sharding import PartitionSpec as P

KSIZE = 7
DILATE = 2
REACH = 6


EPSILON = 1e-06
CONTRACT_ROWS = (((0,), (0,)), ((), ()))
CONTRACT_COLS = (((1,), (1,)), ((), ()))


def normal_cdf(values):
    return 0.5 * (1.0 + jax.scipy.special.erf(values * 0.7071067811865476))


def gelu_exact(values):
    return values * normal_cdf(values)


def gelu_slope(values):
    return normal_cdf(values) + values * jnp.exp(-0.5 * values * values) * 0.3989422804014327


def shift_pairs(count, step):
    if step > 0:
        return [(i, i + 1) for i in range(count - 1)]
    return [(i + 1, i) for i in range(count - 1)]


ROW = ("z", "core")
COL = "col"
EVERY = ("z", "core", "col")


def add_halo(field):
    row_count = lax.axis_size(ROW)
    col_count = lax.axis_size(COL)
    left = lax.ppermute(field[:, -REACH:, :], COL, shift_pairs(col_count, 1))
    right = lax.ppermute(field[:, :REACH, :], COL, shift_pairs(col_count, -1))
    wide = jnp.concatenate([left, field, right], axis=1)
    top = lax.ppermute(wide[-REACH:], ROW, shift_pairs(row_count, 1))
    bottom = lax.ppermute(wide[:REACH], ROW, shift_pairs(row_count, -1))
    return jnp.concatenate([top, wide, bottom], axis=0)


def tile_stencil(padded, tap_table, height, breadth):
    summed = jnp.zeros((height, breadth, tap_table.shape[0]), jnp.float32)
    for tap_row in range(KSIZE):
        for tap_col in range(KSIZE):
            window = padded[
                DILATE * tap_row : DILATE * tap_row + height,
                DILATE * tap_col : DILATE * tap_col + breadth,
                :,
            ].astype(jnp.float32)
            summed = summed + tap_table[:, KSIZE * tap_row + tap_col] * window
    return summed


def tile_taps(padded, gradient, height, breadth):
    columns = []
    for tap_row in range(KSIZE):
        for tap_col in range(KSIZE):
            window = padded[
                DILATE * tap_row : DILATE * tap_row + height,
                DILATE * tap_col : DILATE * tap_col + breadth,
                :,
            ].astype(jnp.float32)
            columns.append(jnp.sum(gradient * window, axis=(0, 1)))
    return jnp.stack(columns, axis=1)


def gather_weights(w_in, w_out):
    row_block, ff = w_in.shape
    core = lax.axis_index("core")
    flat_in = w_in.reshape(-1)
    flat_out = w_out.reshape(-1)
    mine = jnp.where(core == 0, flat_in, flat_out)
    across = lax.all_gather(mine, COL, axis=0, tiled=False)
    both = lax.all_gather(across, "core", axis=0, tiled=False)
    full_in = both[0].reshape(-1, ff)
    full_out = both[1].reshape(-1, w_out.shape[1])
    return full_in, full_out


def reduce_grads(part_in, part_out, small):
    col_count = lax.axis_size(COL)
    rows_in = part_in.shape[0] // col_count
    block_in = part_in.reshape(col_count, -1)
    block_out = part_out.reshape(col_count, -1)
    stacked = jnp.stack([block_in, block_out], axis=1)
    halves = lax.psum_scatter(stacked, "core", scatter_dimension=1, tiled=True)
    halves = halves.reshape(col_count * rows_in, -1)
    mine = lax.psum_scatter(halves, COL, scatter_dimension=0, tiled=True)
    mine = lax.psum(mine, "z")
    pair = lax.all_gather(mine, "core", axis=0, tiled=False).reshape(2, -1)
    grad_in_block = pair[0].reshape(-1, part_in.shape[1])
    grad_out_block = pair[1].reshape(-1, part_out.shape[1])
    small_all = lax.psum(small, EVERY)
    return grad_in_block, grad_out_block, small_all


def local(image, dw_kernel, ln_gain, w_in, b_in, w_out, layer_scale, cotangent):
    tile_rows, tile_cols, channels = image.shape
    hidden_units = w_in.shape[1]
    row_count = lax.axis_size(ROW)
    col_count = lax.axis_size(COL)
    group_count = row_count * col_count
    group_size = channels // group_count
    pixels = tile_rows * tile_cols
    scale_factor = 1.0 / math.sqrt(pixels * group_count)
    full_in, full_out = gather_weights(w_in, w_out)
    flipped = dw_kernel.reshape(channels, KSIZE, KSIZE)[:, ::-1, ::-1].reshape(
        channels, KSIZE * KSIZE
    )
    group_index = lax.axis_index(EVERY)
    padded = add_halo(image)
    conv_tile = tile_stencil(padded, dw_kernel, tile_rows, tile_cols).astype(jnp.bfloat16)
    conv_rows = conv_tile.astype(jnp.float32).reshape(pixels, channels)
    average = jnp.mean(conv_rows, axis=1, keepdims=True)
    centered = conv_rows - average
    inverse = lax.rsqrt(jnp.mean(centered * centered, axis=1, keepdims=True) + EPSILON)
    standard = centered * inverse
    normed = (standard * ln_gain).astype(jnp.bfloat16)
    preact = jnp.dot(normed, full_in, preferred_element_type=jnp.float32) + b_in
    hidden = gelu_exact(preact).astype(jnp.bfloat16)
    mixed = jnp.dot(hidden, full_out, preferred_element_type=jnp.float32)
    out_map = (image.reshape(pixels, channels).astype(jnp.float32) + layer_scale * mixed).astype(
        jnp.bfloat16
    )
    out_map = out_map.reshape(tile_rows, tile_cols, channels)
    upstream = cotangent.reshape(pixels, channels).astype(jnp.float32)
    scale_part = jnp.sum(upstream * mixed, axis=0)
    grad_mix = (upstream * layer_scale).astype(jnp.bfloat16)
    grad_hidden = lax.dot_general(
        grad_mix, full_out, CONTRACT_COLS, preferred_element_type=jnp.float32
    )
    grad_pre = grad_hidden * gelu_slope(preact)
    bias_part = jnp.sum(grad_pre, axis=0)
    grad_pre_rounded = grad_pre.astype(jnp.bfloat16)
    grad_norm = lax.dot_general(
        grad_pre_rounded, full_in, CONTRACT_COLS, preferred_element_type=jnp.float32
    )
    part_in = lax.dot_general(
        normed, grad_pre_rounded, CONTRACT_ROWS, preferred_element_type=jnp.float32
    )
    part_out = lax.dot_general(hidden, grad_mix, CONTRACT_ROWS, preferred_element_type=jnp.float32)
    gain_part = jnp.sum(grad_norm * standard, axis=0)
    scaled = grad_norm * ln_gain
    grad_conv = (
        (
            scaled
            - jnp.mean(scaled, axis=1, keepdims=True)
            - standard * jnp.mean(scaled * standard, axis=1, keepdims=True)
        )
        * inverse
    ).astype(jnp.bfloat16)
    grad_conv = grad_conv.reshape(tile_rows, tile_cols, channels)
    grad_padded = add_halo(grad_conv)
    grad_back = tile_stencil(grad_padded, flipped, tile_rows, tile_cols).astype(jnp.bfloat16)
    kernel_part = tile_taps(padded, grad_conv.astype(jnp.float32), tile_rows, tile_cols)
    grad_image = (cotangent.astype(jnp.float32) + grad_back.astype(jnp.float32)).astype(
        jnp.bfloat16
    )
    small = jnp.concatenate(
        [scale_part, bias_part, gain_part, kernel_part.reshape(-1)]
    )
    grad_in_block, grad_out_block, small_sum = reduce_grads(part_in, part_out, small)
    scale_sum = small_sum[:channels]
    bias_sum = small_sum[channels : channels + hidden_units]
    gain_sum = small_sum[channels + hidden_units : 2 * channels + hidden_units]
    kernel_sum = small_sum[2 * channels + hidden_units : 2 * channels + hidden_units + channels * KSIZE * KSIZE]
    kernel_sum = kernel_sum.reshape(channels, KSIZE * KSIZE)
    grad_kernel = (
        lax.dynamic_slice_in_dim(kernel_sum, group_index * group_size, group_size, 0)
        * scale_factor
    )
    return (
        out_map,
        grad_image,
        grad_kernel,
        grad_in_block * scale_factor,
        grad_out_block * scale_factor,
        bias_sum * scale_factor,
        gain_sum * scale_factor,
        scale_sum * scale_factor,
    )


def solution(mesh):
    devices = mesh.devices.reshape(-1, 2, mesh.devices.shape[1])
    mesh = jax.sharding.Mesh(devices, EVERY)
    tile = P(ROW, COL, None)
    in_specs = (tile, P(), P(), P(COL, None), P(), P(COL, None), P(), tile)
    out_specs = (tile, tile, P(EVERY, None), P(COL, None), P(COL, None), P(), P(), P())
    return jax.shard_map(local, mesh=mesh, in_specs=in_specs, out_specs=out_specs, check_vma=False)
```

```python
import math

import jax
import jax.numpy as jnp
from jax import lax
from jax.sharding import PartitionSpec as P

KSIZE = 7
DILATE = 2
REACH = 6


EPSILON = 1e-06
CONTRACT_ROWS = (((0,), (0,)), ((), ()))
CONTRACT_COLS = (((1,), (1,)), ((), ()))


def normal_cdf(values):
    return 0.5 * (1.0 + jax.scipy.special.erf(values * 0.7071067811865476))


def gelu_exact(values):
    return values * normal_cdf(values)


def gelu_slope(values):
    return normal_cdf(values) + values * jnp.exp(-0.5 * values * values) * 0.3989422804014327


def shift_pairs(count, step):
    if step > 0:
        return [(i, i + 1) for i in range(count - 1)]
    return [(i + 1, i) for i in range(count - 1)]


def add_halo(field):
    row_count = lax.axis_size("row")
    col_count = lax.axis_size("col")
    left = lax.ppermute(field[:, -REACH:, :], "col", shift_pairs(col_count, 1))
    right = lax.ppermute(field[:, :REACH, :], "col", shift_pairs(col_count, -1))
    wide = jnp.concatenate([left, field, right], axis=1)
    top = lax.ppermute(wide[-REACH:], "row", shift_pairs(row_count, 1))
    bottom = lax.ppermute(wide[:REACH], "row", shift_pairs(row_count, -1))
    return jnp.concatenate([top, wide, bottom], axis=0)


def tile_stencil(padded, tap_table, height, breadth):
    summed = jnp.zeros((height, breadth, tap_table.shape[0]), jnp.float32)
    for tap_row in range(KSIZE):
        for tap_col in range(KSIZE):
            window = padded[
                DILATE * tap_row : DILATE * tap_row + height,
                DILATE * tap_col : DILATE * tap_col + breadth,
                :,
            ].astype(jnp.float32)
            summed = summed + tap_table[:, KSIZE * tap_row + tap_col] * window
    return summed


def tile_taps(padded, gradient, height, breadth):
    columns = []
    for tap_row in range(KSIZE):
        for tap_col in range(KSIZE):
            window = padded[
                DILATE * tap_row : DILATE * tap_row + height,
                DILATE * tap_col : DILATE * tap_col + breadth,
                :,
            ].astype(jnp.float32)
            columns.append(jnp.sum(gradient * window, axis=(0, 1)))
    return jnp.stack(columns, axis=1)


def local(image, dw_kernel, ln_gain, w_in, b_in, w_out, layer_scale, cotangent):
    tile_rows, tile_cols, channels = image.shape
    hidden_units = w_in.shape[1]
    row_count = lax.axis_size("row")
    col_count = lax.axis_size("col")
    group_count = row_count * col_count
    group_size = channels // group_count
    pixels = tile_rows * tile_cols
    scale_factor = 1.0 / math.sqrt(pixels * group_count)
    full_in, full_out = (
        lax.all_gather(w_in, "col", axis=0, tiled=True),
        lax.all_gather(w_out, "col", axis=0, tiled=True),
    )
    flipped = dw_kernel.reshape(channels, KSIZE, KSIZE)[:, ::-1, ::-1].reshape(
        channels, KSIZE * KSIZE
    )
    padded = add_halo(image)
    conv_tile = tile_stencil(padded, dw_kernel, tile_rows, tile_cols).astype(jnp.bfloat16)
    conv_rows = conv_tile.astype(jnp.float32).reshape(pixels, channels)
    average = jnp.mean(conv_rows, axis=1, keepdims=True)
    centered = conv_rows - average
    inverse = lax.rsqrt(jnp.mean(centered * centered, axis=1, keepdims=True) + EPSILON)
    standard = centered * inverse
    normed = (standard * ln_gain).astype(jnp.bfloat16)
    preact = jnp.dot(normed, full_in, preferred_element_type=jnp.float32) + b_in
    hidden = gelu_exact(preact).astype(jnp.bfloat16)
    mixed = jnp.dot(hidden, full_out, preferred_element_type=jnp.float32)
    out_map = (image.reshape(pixels, channels).astype(jnp.float32) + layer_scale * mixed).astype(
        jnp.bfloat16
    )
    out_map = out_map.reshape(tile_rows, tile_cols, channels)
    upstream = cotangent.reshape(pixels, channels).astype(jnp.float32)
    scale_part = jnp.sum(upstream * mixed, axis=0)
    grad_mix = (upstream * layer_scale).astype(jnp.bfloat16)
    grad_hidden = lax.dot_general(
        grad_mix, full_out, CONTRACT_COLS, preferred_element_type=jnp.float32
    )
    grad_pre = grad_hidden * gelu_slope(preact)
    bias_part = jnp.sum(grad_pre, axis=0)
    grad_pre_rounded = grad_pre.astype(jnp.bfloat16)
    grad_norm = lax.dot_general(
        grad_pre_rounded, full_in, CONTRACT_COLS, preferred_element_type=jnp.float32
    )
    gain_part = jnp.sum(grad_norm * standard, axis=0)
    scaled = grad_norm * ln_gain
    grad_conv = (
        (
            scaled
            - jnp.mean(scaled, axis=1, keepdims=True)
            - standard * jnp.mean(scaled * standard, axis=1, keepdims=True)
        )
        * inverse
    ).astype(jnp.bfloat16)
    grad_conv = grad_conv.reshape(tile_rows, tile_cols, channels)
    grad_padded = add_halo(grad_conv)
    grad_back = tile_stencil(grad_padded, flipped, tile_rows, tile_cols).astype(jnp.bfloat16)
    kernel_part = tile_taps(padded, grad_conv.astype(jnp.float32), tile_rows, tile_cols)
    grad_image = (cotangent.astype(jnp.float32) + grad_back.astype(jnp.float32)).astype(
        jnp.bfloat16
    )
    gain_part = jnp.sum(grad_norm * standard, axis=0)
    small = jnp.concatenate([bias_part, gain_part, scale_part])
    small = jnp.pad(small, (0, (-small.shape[0]) % (8 * channels))).reshape(-1, channels)
    small_rows = small.shape[0]
    rows_out = hidden_units // col_count
    stacked_out = jnp.concatenate(
        [
            lax.dot_general(
                hidden, grad_mix, CONTRACT_ROWS, preferred_element_type=jnp.float32
            ).reshape(col_count, rows_out, channels),
            jnp.broadcast_to(small[None], (col_count, small_rows, channels)),
        ],
        axis=1,
    ).reshape(-1, channels)
    part_in = lax.psum_scatter(
        lax.dot_general(
            normed, grad_pre_rounded, CONTRACT_ROWS, preferred_element_type=jnp.float32
        ),
        "col",
        scatter_dimension=0,
        tiled=True,
    )
    part_out = lax.psum_scatter(stacked_out, "col", scatter_dimension=0, tiled=True)
    summed_in, summed_out = lax.psum((part_in, part_out), "row")
    small_sum = summed_out[rows_out:].reshape(-1)
    summed_out = summed_out[:rows_out]
    bias_sum = small_sum[:hidden_units]
    gain_sum = small_sum[hidden_units : hidden_units + channels]
    scale_sum = small_sum[hidden_units + channels : hidden_units + 2 * channels]
    kernel_parts = lax.all_to_all(
        kernel_part.reshape(group_count, group_size, KSIZE * KSIZE),
        ("row", "col"),
        split_axis=0,
        concat_axis=0,
        tiled=True,
    )
    grad_kernel = jnp.sum(kernel_parts, axis=0) * scale_factor
    return (
        out_map,
        grad_image,
        grad_kernel,
        summed_in * scale_factor,
        summed_out * scale_factor,
        bias_sum * scale_factor,
        gain_sum * scale_factor,
        scale_sum * scale_factor,
    )


def solution(mesh):
    in_specs = (
        P("row", "col", None),
        P(),
        P(),
        P("col", None),
        P(),
        P("col", None),
        P(),
        P("row", "col", None),
    )
    out_specs = (
        P("row", "col", None),
        P("row", "col", None),
        P(("row", "col"), None),
        P("col", None),
        P("col", None),
        P(),
        P(),
        P(),
    )
    return jax.shard_map(local, mesh=mesh, in_specs=in_specs, out_specs=out_specs, check_vma=False)
```

```python
import math

import jax
import jax.numpy as jnp
from jax import lax
from jax.sharding import PartitionSpec as P

KSIZE = 7
DILATE = 2
REACH = 6


EPSILON = 1e-06
CONTRACT_ROWS = (((0,), (0,)), ((), ()))
CONTRACT_COLS = (((1,), (1,)), ((), ()))


def normal_cdf(values):
    return 0.5 * (1.0 + jax.scipy.special.erf(values * 0.7071067811865476))


def gelu_exact(values):
    return values * normal_cdf(values)


def gelu_slope(values):
    return normal_cdf(values) + values * jnp.exp(-0.5 * values * values) * 0.3989422804014327


def shift_pairs(count, step):
    if step > 0:
        return [(i, i + 1) for i in range(count - 1)]
    return [(i + 1, i) for i in range(count - 1)]


def add_halo(field):
    row_count = lax.axis_size("row")
    col_count = lax.axis_size("col")
    left = lax.ppermute(field[:, -REACH:, :], "col", shift_pairs(col_count, 1))
    right = lax.ppermute(field[:, :REACH, :], "col", shift_pairs(col_count, -1))
    wide = jnp.concatenate([left, field, right], axis=1)
    top = lax.ppermute(wide[-REACH:], "row", shift_pairs(row_count, 1))
    bottom = lax.ppermute(wide[:REACH], "row", shift_pairs(row_count, -1))
    return jnp.concatenate([top, wide, bottom], axis=0)


def tile_stencil(padded, tap_table, height, breadth):
    summed = jnp.zeros((height, breadth, tap_table.shape[0]), jnp.float32)
    for tap_row in range(KSIZE):
        for tap_col in range(KSIZE):
            window = padded[
                DILATE * tap_row : DILATE * tap_row + height,
                DILATE * tap_col : DILATE * tap_col + breadth,
                :,
            ].astype(jnp.float32)
            summed = summed + tap_table[:, KSIZE * tap_row + tap_col] * window
    return summed


def tile_taps(padded, gradient, height, breadth):
    columns = []
    for tap_row in range(KSIZE):
        for tap_col in range(KSIZE):
            window = padded[
                DILATE * tap_row : DILATE * tap_row + height,
                DILATE * tap_col : DILATE * tap_col + breadth,
                :,
            ].astype(jnp.float32)
            columns.append(jnp.sum(gradient * window, axis=(0, 1)))
    return jnp.stack(columns, axis=1)


def local(image, dw_kernel, ln_gain, w_in, b_in, w_out, layer_scale, cotangent):
    tile_rows, tile_cols, channels = image.shape
    hidden_units = w_in.shape[1]
    row_count = lax.axis_size("row")
    col_count = lax.axis_size("col")
    group_count = row_count * col_count
    group_size = channels // group_count
    pixels = tile_rows * tile_cols
    scale_factor = 1.0 / math.sqrt(pixels * group_count)
    full_in = lax.all_gather(w_in, "col", axis=0, tiled=True)
    full_out = lax.all_to_all(
        jnp.broadcast_to(w_out[None], (col_count,) + w_out.shape),
        "col",
        split_axis=0,
        concat_axis=0,
        tiled=True,
    ).reshape(-1, channels)
    flipped = dw_kernel.reshape(channels, KSIZE, KSIZE)[:, ::-1, ::-1].reshape(
        channels, KSIZE * KSIZE
    )
    padded = add_halo(image)
    conv_tile = tile_stencil(padded, dw_kernel, tile_rows, tile_cols).astype(jnp.bfloat16)
    conv_rows = conv_tile.astype(jnp.float32).reshape(pixels, channels)
    average = jnp.mean(conv_rows, axis=1, keepdims=True)
    centered = conv_rows - average
    inverse = lax.rsqrt(jnp.mean(centered * centered, axis=1, keepdims=True) + EPSILON)
    standard = centered * inverse
    normed = (standard * ln_gain).astype(jnp.bfloat16)
    preact = jnp.dot(normed, full_in, preferred_element_type=jnp.float32) + b_in
    hidden = gelu_exact(preact).astype(jnp.bfloat16)
    mixed = jnp.dot(hidden, full_out, preferred_element_type=jnp.float32)
    out_map = (image.reshape(pixels, channels).astype(jnp.float32) + layer_scale * mixed).astype(
        jnp.bfloat16
    )
    out_map = out_map.reshape(tile_rows, tile_cols, channels)
    upstream = cotangent.reshape(pixels, channels).astype(jnp.float32)
    scale_part = jnp.sum(upstream * mixed, axis=0)
    grad_mix = (upstream * layer_scale).astype(jnp.bfloat16)
    grad_hidden = lax.dot_general(
        grad_mix, full_out, CONTRACT_COLS, preferred_element_type=jnp.float32
    )
    grad_pre = grad_hidden * gelu_slope(preact)
    bias_part = jnp.sum(grad_pre, axis=0)
    grad_pre_rounded = grad_pre.astype(jnp.bfloat16)
    grad_norm = lax.dot_general(
        grad_pre_rounded, full_in, CONTRACT_COLS, preferred_element_type=jnp.float32
    )
    gain_part = jnp.sum(grad_norm * standard, axis=0)
    scaled = grad_norm * ln_gain
    grad_conv = (
        (
            scaled
            - jnp.mean(scaled, axis=1, keepdims=True)
            - standard * jnp.mean(scaled * standard, axis=1, keepdims=True)
        )
        * inverse
    ).astype(jnp.bfloat16)
    grad_conv = grad_conv.reshape(tile_rows, tile_cols, channels)
    grad_padded = add_halo(grad_conv)
    grad_back = tile_stencil(grad_padded, flipped, tile_rows, tile_cols).astype(jnp.bfloat16)
    kernel_part = tile_taps(padded, grad_conv.astype(jnp.float32), tile_rows, tile_cols)
    grad_image = (cotangent.astype(jnp.float32) + grad_back.astype(jnp.float32)).astype(
        jnp.bfloat16
    )
    gain_part = jnp.sum(grad_norm * standard, axis=0)
    small = jnp.concatenate([bias_part, gain_part, scale_part])
    small = jnp.pad(small, (0, (-small.shape[0]) % (8 * channels))).reshape(-1, channels)
    small_rows = small.shape[0]
    rows_out = hidden_units // col_count
    stacked_out = jnp.concatenate(
        [
            lax.dot_general(
                hidden, grad_mix, CONTRACT_ROWS, preferred_element_type=jnp.float32
            ).reshape(col_count, rows_out, channels),
            jnp.broadcast_to(small[None], (col_count, small_rows, channels)),
        ],
        axis=1,
    ).reshape(-1, channels)
    part_in = lax.psum_scatter(
        lax.dot_general(
            normed, grad_pre_rounded, CONTRACT_ROWS, preferred_element_type=jnp.float32
        ),
        "col",
        scatter_dimension=0,
        tiled=True,
    )
    part_out = jnp.sum(
        lax.all_to_all(
            stacked_out.reshape(col_count, -1, channels),
            "col",
            split_axis=0,
            concat_axis=0,
            tiled=True,
        ),
        axis=0,
    )
    summed_in, summed_out = lax.psum((part_in, part_out), "row")
    small_sum = summed_out[rows_out:].reshape(-1)
    summed_out = summed_out[:rows_out]
    bias_sum = small_sum[:hidden_units]
    gain_sum = small_sum[hidden_units : hidden_units + channels]
    scale_sum = small_sum[hidden_units + channels : hidden_units + 2 * channels]
    kernel_parts = lax.all_to_all(
        kernel_part.reshape(group_count, group_size, KSIZE * KSIZE),
        ("row", "col"),
        split_axis=0,
        concat_axis=0,
        tiled=True,
    )
    grad_kernel = jnp.sum(kernel_parts, axis=0) * scale_factor
    return (
        out_map,
        grad_image,
        grad_kernel,
        summed_in * scale_factor,
        summed_out * scale_factor,
        bias_sum * scale_factor,
        gain_sum * scale_factor,
        scale_sum * scale_factor,
    )


def solution(mesh):
    in_specs = (
        P("row", "col", None),
        P(),
        P(),
        P("col", None),
        P(),
        P("col", None),
        P(),
        P("row", "col", None),
    )
    out_specs = (
        P("row", "col", None),
        P("row", "col", None),
        P(("row", "col"), None),
        P("col", None),
        P("col", None),
        P(),
        P(),
        P(),
    )
    return jax.shard_map(local, mesh=mesh, in_specs=in_specs, out_specs=out_specs, check_vma=False)
```

```python
import math

import jax
import jax.numpy as jnp
from jax import lax
from jax.sharding import PartitionSpec as P

KSIZE = 7
DILATE = 2
REACH = 6


EPSILON = 1e-06
CONTRACT_ROWS = (((0,), (0,)), ((), ()))
CONTRACT_COLS = (((1,), (1,)), ((), ()))


def normal_cdf(values):
    return 0.5 * (1.0 + jax.scipy.special.erf(values * 0.7071067811865476))


def gelu_exact(values):
    return values * normal_cdf(values)


def gelu_slope(values):
    return normal_cdf(values) + values * jnp.exp(-0.5 * values * values) * 0.3989422804014327


def shift_pairs(count, step):
    if step > 0:
        return [(i, i + 1) for i in range(count - 1)]
    return [(i + 1, i) for i in range(count - 1)]


ROW = ("z", "core")
EVERY = ("z", "core", "col")


def add_halo(field):
    row_count = lax.axis_size(ROW)
    col_count = lax.axis_size("col")
    left = lax.ppermute(field[:, -REACH:, :], "col", shift_pairs(col_count, 1))
    right = lax.ppermute(field[:, :REACH, :], "col", shift_pairs(col_count, -1))
    wide = jnp.concatenate([left, field, right], axis=1)
    top = lax.ppermute(wide[-REACH:], ROW, shift_pairs(row_count, 1))
    bottom = lax.ppermute(wide[:REACH], ROW, shift_pairs(row_count, -1))
    return jnp.concatenate([top, wide, bottom], axis=0)


def tile_stencil(padded, tap_table, height, breadth):
    summed = jnp.zeros((height, breadth, tap_table.shape[0]), jnp.float32)
    for tap_row in range(KSIZE):
        for tap_col in range(KSIZE):
            window = padded[
                DILATE * tap_row : DILATE * tap_row + height,
                DILATE * tap_col : DILATE * tap_col + breadth,
                :,
            ].astype(jnp.float32)
            summed = summed + tap_table[:, KSIZE * tap_row + tap_col] * window
    return summed


def tile_taps(padded, gradient, height, breadth):
    columns = []
    for tap_row in range(KSIZE):
        for tap_col in range(KSIZE):
            window = padded[
                DILATE * tap_row : DILATE * tap_row + height,
                DILATE * tap_col : DILATE * tap_col + breadth,
                :,
            ].astype(jnp.float32)
            columns.append(jnp.sum(gradient * window, axis=(0, 1)))
    return jnp.stack(columns, axis=1)


def local(image, dw_kernel, ln_gain, w_in, b_in, w_out, layer_scale, cotangent):
    tile_rows, tile_cols, channels = image.shape
    hidden_units = w_in.shape[1]
    row_count = lax.axis_size(ROW)
    col_count = lax.axis_size("col")
    group_count = row_count * col_count
    group_size = channels // group_count
    pixels = tile_rows * tile_cols
    scale_factor = 1.0 / math.sqrt(pixels * group_count)
    full_in, full_out = (
        lax.all_gather(w_in, "col", axis=0, tiled=True),
        lax.all_gather(w_out, "col", axis=0, tiled=True),
    )
    flipped = dw_kernel.reshape(channels, KSIZE, KSIZE)[:, ::-1, ::-1].reshape(
        channels, KSIZE * KSIZE
    )
    padded = add_halo(image)
    conv_tile = tile_stencil(padded, dw_kernel, tile_rows, tile_cols).astype(jnp.bfloat16)
    conv_rows = conv_tile.astype(jnp.float32).reshape(pixels, channels)
    average = jnp.mean(conv_rows, axis=1, keepdims=True)
    centered = conv_rows - average
    inverse = lax.rsqrt(jnp.mean(centered * centered, axis=1, keepdims=True) + EPSILON)
    standard = centered * inverse
    normed = (standard * ln_gain).astype(jnp.bfloat16)
    preact = jnp.dot(normed, full_in, preferred_element_type=jnp.float32) + b_in
    hidden = gelu_exact(preact).astype(jnp.bfloat16)
    mixed = jnp.dot(hidden, full_out, preferred_element_type=jnp.float32)
    out_map = (image.reshape(pixels, channels).astype(jnp.float32) + layer_scale * mixed).astype(
        jnp.bfloat16
    )
    out_map = out_map.reshape(tile_rows, tile_cols, channels)
    upstream = cotangent.reshape(pixels, channels).astype(jnp.float32)
    scale_part = jnp.sum(upstream * mixed, axis=0)
    grad_mix = (upstream * layer_scale).astype(jnp.bfloat16)
    grad_hidden = lax.dot_general(
        grad_mix, full_out, CONTRACT_COLS, preferred_element_type=jnp.float32
    )
    grad_pre = grad_hidden * gelu_slope(preact)
    bias_part = jnp.sum(grad_pre, axis=0)
    grad_pre_rounded = grad_pre.astype(jnp.bfloat16)
    grad_norm = lax.dot_general(
        grad_pre_rounded, full_in, CONTRACT_COLS, preferred_element_type=jnp.float32
    )
    gain_part = jnp.sum(grad_norm * standard, axis=0)
    scaled = grad_norm * ln_gain
    grad_conv = (
        (
            scaled
            - jnp.mean(scaled, axis=1, keepdims=True)
            - standard * jnp.mean(scaled * standard, axis=1, keepdims=True)
        )
        * inverse
    ).astype(jnp.bfloat16)
    grad_conv = grad_conv.reshape(tile_rows, tile_cols, channels)
    grad_padded = add_halo(grad_conv)
    grad_back = tile_stencil(grad_padded, flipped, tile_rows, tile_cols).astype(jnp.bfloat16)
    kernel_part = tile_taps(padded, grad_conv.astype(jnp.float32), tile_rows, tile_cols)
    grad_image = (cotangent.astype(jnp.float32) + grad_back.astype(jnp.float32)).astype(
        jnp.bfloat16
    )
    gain_part = jnp.sum(grad_norm * standard, axis=0)
    small = jnp.concatenate([bias_part, gain_part, scale_part])
    small = jnp.pad(small, (0, (-small.shape[0]) % (8 * channels))).reshape(-1, channels)
    small_rows = small.shape[0]
    rows_out = hidden_units // col_count
    block_in = lax.dot_general(
        normed, grad_pre_rounded, CONTRACT_ROWS, preferred_element_type=jnp.float32
    ).reshape(col_count, rows_out, channels)
    block_out = lax.dot_general(
        hidden, grad_mix, CONTRACT_ROWS, preferred_element_type=jnp.float32
    ).reshape(col_count, rows_out, channels)
    block_in = jnp.concatenate(
        [block_in, jnp.zeros((col_count, small_rows, channels), jnp.float32)], axis=1
    )
    block_out = jnp.concatenate(
        [block_out, jnp.broadcast_to(small[None], (col_count, small_rows, channels))], axis=1
    )
    stacked = jnp.stack([block_in, block_out], axis=1)
    halves = lax.psum_scatter(stacked, "core", scatter_dimension=1, tiled=True)
    halves = halves.reshape(-1, channels)
    mine = lax.psum_scatter(halves, "col", scatter_dimension=0, tiled=True)
    mine = lax.psum(mine, "z")
    pair = lax.all_gather(mine, "core", axis=0, tiled=False)
    summed_in = pair[0, :rows_out].reshape(-1, hidden_units)
    summed_out = pair[1, :rows_out]
    small_sum = pair[1, rows_out:].reshape(-1)
    bias_sum = small_sum[:hidden_units]
    gain_sum = small_sum[hidden_units : hidden_units + channels]
    scale_sum = small_sum[hidden_units + channels : hidden_units + 2 * channels]
    kernel_parts = lax.all_to_all(
        kernel_part.reshape(group_count, group_size, KSIZE * KSIZE),
        EVERY,
        split_axis=0,
        concat_axis=0,
        tiled=True,
    )
    grad_kernel = jnp.sum(kernel_parts, axis=0) * scale_factor
    return (
        out_map,
        grad_image,
        grad_kernel,
        summed_in * scale_factor,
        summed_out * scale_factor,
        bias_sum * scale_factor,
        gain_sum * scale_factor,
        scale_sum * scale_factor,
    )


def solution(mesh):
    devices = mesh.devices.reshape(-1, 2, mesh.devices.shape[1])
    mesh = jax.sharding.Mesh(devices, EVERY)
    tile = P(ROW, "col", None)
    in_specs = (tile, P(), P(), P("col", None), P(), P("col", None), P(), tile)
    out_specs = (tile, tile, P(EVERY, None), P("col", None), P("col", None), P(), P(), P())
    return jax.shard_map(local, mesh=mesh, in_specs=in_specs, out_specs=out_specs, check_vma=False)
```

```python
import math

import jax
import jax.numpy as jnp
from jax import lax
from jax.sharding import PartitionSpec as P

KSIZE = 7
DILATE = 2
REACH = 6


EPSILON = 1e-06
CONTRACT_ROWS = (((0,), (0,)), ((), ()))
CONTRACT_COLS = (((1,), (1,)), ((), ()))


def normal_cdf(values):
    return 0.5 * (1.0 + jax.scipy.special.erf(values * 0.7071067811865476))


def gelu_exact(values):
    return values * normal_cdf(values)


def gelu_slope(values):
    return normal_cdf(values) + values * jnp.exp(-0.5 * values * values) * 0.3989422804014327


def shift_pairs(count, step):
    if step > 0:
        return [(i, i + 1) for i in range(count - 1)]
    return [(i + 1, i) for i in range(count - 1)]


ROW = ("z", "core")
EVERY = ("z", "core", "col")


def add_halo(field):
    row_count = lax.axis_size(ROW)
    col_count = lax.axis_size("col")
    left = lax.ppermute(field[:, -REACH:, :], "col", shift_pairs(col_count, 1))
    right = lax.ppermute(field[:, :REACH, :], "col", shift_pairs(col_count, -1))
    wide = jnp.concatenate([left, field, right], axis=1)
    top = lax.ppermute(wide[-REACH:], ROW, shift_pairs(row_count, 1))
    bottom = lax.ppermute(wide[:REACH], ROW, shift_pairs(row_count, -1))
    return jnp.concatenate([top, wide, bottom], axis=0)


def tile_stencil(padded, tap_table, height, breadth):
    summed = jnp.zeros((height, breadth, tap_table.shape[0]), jnp.float32)
    for tap_row in range(KSIZE):
        for tap_col in range(KSIZE):
            window = padded[
                DILATE * tap_row : DILATE * tap_row + height,
                DILATE * tap_col : DILATE * tap_col + breadth,
                :,
            ].astype(jnp.float32)
            summed = summed + tap_table[:, KSIZE * tap_row + tap_col] * window
    return summed


def tile_taps(padded, gradient, height, breadth):
    columns = []
    for tap_row in range(KSIZE):
        for tap_col in range(KSIZE):
            window = padded[
                DILATE * tap_row : DILATE * tap_row + height,
                DILATE * tap_col : DILATE * tap_col + breadth,
                :,
            ].astype(jnp.float32)
            columns.append(jnp.sum(gradient * window, axis=(0, 1)))
    return jnp.stack(columns, axis=1)


def local(image, dw_kernel, ln_gain, w_in, b_in, w_out, layer_scale, cotangent):
    tile_rows, tile_cols, channels = image.shape
    hidden_units = w_in.shape[1]
    row_count = lax.axis_size(ROW)
    col_count = lax.axis_size("col")
    group_count = row_count * col_count
    group_size = channels // group_count
    pixels = tile_rows * tile_cols
    scale_factor = 1.0 / math.sqrt(pixels * group_count)
    full_in, full_out = (
        lax.all_gather(w_in, "col", axis=0, tiled=True),
        lax.all_gather(w_out, "col", axis=0, tiled=True),
    )
    flipped = dw_kernel.reshape(channels, KSIZE, KSIZE)[:, ::-1, ::-1].reshape(
        channels, KSIZE * KSIZE
    )
    padded = add_halo(image)
    conv_tile = tile_stencil(padded, dw_kernel, tile_rows, tile_cols).astype(jnp.bfloat16)
    conv_rows = conv_tile.astype(jnp.float32).reshape(pixels, channels)
    average = jnp.mean(conv_rows, axis=1, keepdims=True)
    centered = conv_rows - average
    inverse = lax.rsqrt(jnp.mean(centered * centered, axis=1, keepdims=True) + EPSILON)
    standard = centered * inverse
    normed = (standard * ln_gain).astype(jnp.bfloat16)
    preact = jnp.dot(normed, full_in, preferred_element_type=jnp.float32) + b_in
    hidden = gelu_exact(preact).astype(jnp.bfloat16)
    mixed = jnp.dot(hidden, full_out, preferred_element_type=jnp.float32)
    out_map = (image.reshape(pixels, channels).astype(jnp.float32) + layer_scale * mixed).astype(
        jnp.bfloat16
    )
    out_map = out_map.reshape(tile_rows, tile_cols, channels)
    upstream = cotangent.reshape(pixels, channels).astype(jnp.float32)
    scale_part = jnp.sum(upstream * mixed, axis=0)
    grad_mix = (upstream * layer_scale).astype(jnp.bfloat16)
    grad_hidden = lax.dot_general(
        grad_mix, full_out, CONTRACT_COLS, preferred_element_type=jnp.float32
    )
    grad_pre = grad_hidden * gelu_slope(preact)
    bias_part = jnp.sum(grad_pre, axis=0)
    grad_pre_rounded = grad_pre.astype(jnp.bfloat16)
    grad_norm = lax.dot_general(
        grad_pre_rounded, full_in, CONTRACT_COLS, preferred_element_type=jnp.float32
    )
    gain_part = jnp.sum(grad_norm * standard, axis=0)
    scaled = grad_norm * ln_gain
    grad_conv = (
        (
            scaled
            - jnp.mean(scaled, axis=1, keepdims=True)
            - standard * jnp.mean(scaled * standard, axis=1, keepdims=True)
        )
        * inverse
    ).astype(jnp.bfloat16)
    grad_conv = grad_conv.reshape(tile_rows, tile_cols, channels)
    grad_padded = add_halo(grad_conv)
    grad_back = tile_stencil(grad_padded, flipped, tile_rows, tile_cols).astype(jnp.bfloat16)
    kernel_part = tile_taps(padded, grad_conv.astype(jnp.float32), tile_rows, tile_cols)
    grad_image = (cotangent.astype(jnp.float32) + grad_back.astype(jnp.float32)).astype(
        jnp.bfloat16
    )
    gain_part = jnp.sum(grad_norm * standard, axis=0)
    small = jnp.concatenate([bias_part, gain_part, scale_part])
    small = jnp.pad(small, (0, (-small.shape[0]) % (16 * channels))).reshape(-1, channels)
    small_rows = small.shape[0]
    rows_out = hidden_units // col_count
    rows_in = channels // col_count
    block_out = lax.dot_general(
        hidden, grad_mix, CONTRACT_ROWS, preferred_element_type=jnp.float32
    ).reshape(col_count, rows_out, channels)
    block_out = jnp.concatenate(
        [block_out, jnp.broadcast_to(small[None], (col_count, small_rows, channels))], axis=1
    )
    half_out = lax.psum_scatter(block_out, "core", scatter_dimension=1, tiled=True)
    mine_out = lax.psum_scatter(
        half_out.reshape(-1, channels), "col", scatter_dimension=0, tiled=True
    )
    block_in = lax.dot_general(
        normed, grad_pre_rounded, CONTRACT_ROWS, preferred_element_type=jnp.float32
    ).reshape(col_count, rows_in, hidden_units)
    half_in = lax.psum_scatter(block_in, "core", scatter_dimension=2, tiled=True)
    mine_in = lax.psum_scatter(
        half_in.reshape(col_count * rows_in, -1), "col", scatter_dimension=0, tiled=True
    )
    mine_in, mine_out = lax.psum((mine_in, mine_out), "z")
    pair_in, pair_out = lax.all_gather((mine_in, mine_out), "core", axis=0, tiled=False)
    summed_in = jnp.concatenate([pair_in[0], pair_in[1]], axis=1)
    whole_out = pair_out.reshape(-1, channels)
    summed_out = whole_out[:rows_out]
    small_sum = whole_out[rows_out:].reshape(-1)
    bias_sum = small_sum[:hidden_units]
    gain_sum = small_sum[hidden_units : hidden_units + channels]
    scale_sum = small_sum[hidden_units + channels : hidden_units + 2 * channels]
    kernel_parts = lax.all_to_all(
        kernel_part.reshape(group_count, group_size, KSIZE * KSIZE),
        EVERY,
        split_axis=0,
        concat_axis=0,
        tiled=True,
    )
    grad_kernel = jnp.sum(kernel_parts, axis=0) * scale_factor
    return (
        out_map,
        grad_image,
        grad_kernel,
        summed_in * scale_factor,
        summed_out * scale_factor,
        bias_sum * scale_factor,
        gain_sum * scale_factor,
        scale_sum * scale_factor,
    )


def solution(mesh):
    devices = mesh.devices.reshape(-1, 2, mesh.devices.shape[1])
    mesh = jax.sharding.Mesh(devices, EVERY)
    tile = P(ROW, "col", None)
    in_specs = (tile, P(), P(), P("col", None), P(), P("col", None), P(), tile)
    out_specs = (tile, tile, P(EVERY, None), P("col", None), P("col", None), P(), P(), P())
    return jax.shard_map(local, mesh=mesh, in_specs=in_specs, out_specs=out_specs, check_vma=False)
```

```python
import math

import jax
import jax.numpy as jnp
from jax import lax
from jax.sharding import PartitionSpec as P

KSIZE = 7
DILATE = 2
REACH = 6


EPSILON = 1e-06
CONTRACT_ROWS = (((0,), (0,)), ((), ()))
CONTRACT_COLS = (((1,), (1,)), ((), ()))


def normal_cdf(values):
    return 0.5 * (1.0 + jax.scipy.special.erf(values * 0.7071067811865476))


def gelu_exact(values):
    return values * normal_cdf(values)


def gelu_slope(values):
    return normal_cdf(values) + values * jnp.exp(-0.5 * values * values) * 0.3989422804014327


def shift_pairs(count, step):
    if step > 0:
        return [(i, i + 1) for i in range(count - 1)]
    return [(i + 1, i) for i in range(count - 1)]


ROW = ("z", "core")
EVERY = ("z", "core", "col")


def add_halo(field):
    row_count = lax.axis_size(ROW)
    col_count = lax.axis_size("col")
    left = lax.ppermute(field[:, -REACH:, :], "col", shift_pairs(col_count, 1))
    right = lax.ppermute(field[:, :REACH, :], "col", shift_pairs(col_count, -1))
    wide = jnp.concatenate([left, field, right], axis=1)
    top = lax.ppermute(wide[-REACH:], ROW, shift_pairs(row_count, 1))
    bottom = lax.ppermute(wide[:REACH], ROW, shift_pairs(row_count, -1))
    return jnp.concatenate([top, wide, bottom], axis=0)


def tile_stencil(padded, tap_table, height, breadth):
    summed = jnp.zeros((height, breadth, tap_table.shape[0]), jnp.float32)
    for tap_row in range(KSIZE):
        for tap_col in range(KSIZE):
            window = padded[
                DILATE * tap_row : DILATE * tap_row + height,
                DILATE * tap_col : DILATE * tap_col + breadth,
                :,
            ].astype(jnp.float32)
            summed = summed + tap_table[:, KSIZE * tap_row + tap_col] * window
    return summed


def tile_taps(padded, gradient, height, breadth):
    columns = []
    for tap_row in range(KSIZE):
        for tap_col in range(KSIZE):
            window = padded[
                DILATE * tap_row : DILATE * tap_row + height,
                DILATE * tap_col : DILATE * tap_col + breadth,
                :,
            ].astype(jnp.float32)
            columns.append(jnp.sum(gradient * window, axis=(0, 1)))
    return jnp.stack(columns, axis=1)


def local(image, dw_kernel, ln_gain, w_in, b_in, w_out, layer_scale, cotangent):
    tile_rows, tile_cols, channels = image.shape
    hidden_units = w_in.shape[1]
    row_count = lax.axis_size(ROW)
    col_count = lax.axis_size("col")
    group_count = row_count * col_count
    group_size = channels // group_count
    pixels = tile_rows * tile_cols
    scale_factor = 1.0 / math.sqrt(pixels * group_count)
    shards = jnp.concatenate([w_in.reshape(-1, channels), w_out], axis=0)
    gathered = lax.all_gather(shards, "col", axis=0, tiled=False)
    in_rows = w_in.shape[0] * hidden_units // channels
    full_in = gathered[:, :in_rows].reshape(-1, hidden_units)
    full_out = gathered[:, in_rows:].reshape(-1, channels)
    flipped = dw_kernel.reshape(channels, KSIZE, KSIZE)[:, ::-1, ::-1].reshape(
        channels, KSIZE * KSIZE
    )
    padded = add_halo(image)
    conv_tile = tile_stencil(padded, dw_kernel, tile_rows, tile_cols).astype(jnp.bfloat16)
    conv_rows = conv_tile.astype(jnp.float32).reshape(pixels, channels)
    average = jnp.mean(conv_rows, axis=1, keepdims=True)
    centered = conv_rows - average
    inverse = lax.rsqrt(jnp.mean(centered * centered, axis=1, keepdims=True) + EPSILON)
    standard = centered * inverse
    normed = (standard * ln_gain).astype(jnp.bfloat16)
    preact = jnp.dot(normed, full_in, preferred_element_type=jnp.float32) + b_in
    hidden = gelu_exact(preact).astype(jnp.bfloat16)
    mixed = jnp.dot(hidden, full_out, preferred_element_type=jnp.float32)
    out_map = (image.reshape(pixels, channels).astype(jnp.float32) + layer_scale * mixed).astype(
        jnp.bfloat16
    )
    out_map = out_map.reshape(tile_rows, tile_cols, channels)
    upstream = cotangent.reshape(pixels, channels).astype(jnp.float32)
    scale_part = jnp.sum(upstream * mixed, axis=0)
    grad_mix = (upstream * layer_scale).astype(jnp.bfloat16)
    grad_hidden = lax.dot_general(
        grad_mix, full_out, CONTRACT_COLS, preferred_element_type=jnp.float32
    )
    grad_pre = grad_hidden * gelu_slope(preact)
    bias_part = jnp.sum(grad_pre, axis=0)
    grad_pre_rounded = grad_pre.astype(jnp.bfloat16)
    grad_norm = lax.dot_general(
        grad_pre_rounded, full_in, CONTRACT_COLS, preferred_element_type=jnp.float32
    )
    gain_part = jnp.sum(grad_norm * standard, axis=0)
    scaled = grad_norm * ln_gain
    grad_conv = (
        (
            scaled
            - jnp.mean(scaled, axis=1, keepdims=True)
            - standard * jnp.mean(scaled * standard, axis=1, keepdims=True)
        )
        * inverse
    ).astype(jnp.bfloat16)
    grad_conv = grad_conv.reshape(tile_rows, tile_cols, channels)
    grad_padded = add_halo(grad_conv)
    grad_back = tile_stencil(grad_padded, flipped, tile_rows, tile_cols).astype(jnp.bfloat16)
    kernel_part = tile_taps(padded, grad_conv.astype(jnp.float32), tile_rows, tile_cols)
    grad_image = (cotangent.astype(jnp.float32) + grad_back.astype(jnp.float32)).astype(
        jnp.bfloat16
    )
    gain_part = jnp.sum(grad_norm * standard, axis=0)
    small = jnp.concatenate([bias_part, gain_part, scale_part])
    small = jnp.pad(small, (0, (-small.shape[0]) % (8 * channels))).reshape(-1, channels)
    small_rows = small.shape[0]
    rows_out = hidden_units // col_count
    block_in = lax.dot_general(
        normed, grad_pre_rounded, CONTRACT_ROWS, preferred_element_type=jnp.float32
    ).reshape(col_count, rows_out, channels)
    block_out = lax.dot_general(
        hidden, grad_mix, CONTRACT_ROWS, preferred_element_type=jnp.float32
    ).reshape(col_count, rows_out, channels)
    block_in = jnp.concatenate(
        [block_in, jnp.zeros((col_count, small_rows, channels), jnp.float32)], axis=1
    )
    block_out = jnp.concatenate(
        [block_out, jnp.broadcast_to(small[None], (col_count, small_rows, channels))], axis=1
    )
    stacked = jnp.stack([block_in, block_out], axis=1)
    halves = lax.psum_scatter(stacked, "core", scatter_dimension=1, tiled=True)
    halves = halves.reshape(-1, channels)
    mine = lax.psum_scatter(halves, "col", scatter_dimension=0, tiled=True)
    mine = lax.psum(mine, "z")
    pair = lax.all_gather(mine, "core", axis=0, tiled=False)
    summed_in = pair[0, :rows_out].reshape(-1, hidden_units)
    summed_out = pair[1, :rows_out]
    small_sum = pair[1, rows_out:].reshape(-1)
    bias_sum = small_sum[:hidden_units]
    gain_sum = small_sum[hidden_units : hidden_units + channels]
    scale_sum = small_sum[hidden_units + channels : hidden_units + 2 * channels]
    kernel_parts = lax.all_to_all(
        kernel_part.reshape(group_count, group_size, KSIZE * KSIZE),
        EVERY,
        split_axis=0,
        concat_axis=0,
        tiled=True,
    )
    grad_kernel = jnp.sum(kernel_parts, axis=0) * scale_factor
    return (
        out_map,
        grad_image,
        grad_kernel,
        summed_in * scale_factor,
        summed_out * scale_factor,
        bias_sum * scale_factor,
        gain_sum * scale_factor,
        scale_sum * scale_factor,
    )


def solution(mesh):
    devices = mesh.devices.reshape(-1, 2, mesh.devices.shape[1])
    mesh = jax.sharding.Mesh(devices, EVERY)
    tile = P(ROW, "col", None)
    in_specs = (tile, P(), P(), P("col", None), P(), P("col", None), P(), tile)
    out_specs = (tile, tile, P(EVERY, None), P("col", None), P("col", None), P(), P(), P())
    return jax.shard_map(local, mesh=mesh, in_specs=in_specs, out_specs=out_specs, check_vma=False)
```

```python
import math

import jax
import jax.numpy as jnp
from jax import lax
from jax.sharding import PartitionSpec as P

KSIZE = 7
DILATE = 2
REACH = 6


EPSILON = 1e-06
CONTRACT_ROWS = (((0,), (0,)), ((), ()))
CONTRACT_COLS = (((1,), (1,)), ((), ()))


def normal_cdf(values):
    return 0.5 * (1.0 + jax.scipy.special.erf(values * 0.7071067811865476))


def gelu_exact(values):
    return values * normal_cdf(values)


def gelu_slope(values):
    return normal_cdf(values) + values * jnp.exp(-0.5 * values * values) * 0.3989422804014327


def shift_pairs(count, step):
    if step > 0:
        return [(i, i + 1) for i in range(count - 1)]
    return [(i + 1, i) for i in range(count - 1)]


ROW = ("z", "core")
EVERY = ("z", "core", "col")


def add_halo(field):
    row_count = lax.axis_size(ROW)
    col_count = lax.axis_size("col")
    left = lax.ppermute(field[:, -REACH:, :], "col", shift_pairs(col_count, 1))
    right = lax.ppermute(field[:, :REACH, :], "col", shift_pairs(col_count, -1))
    wide = jnp.concatenate([left, field, right], axis=1)
    top = lax.ppermute(wide[-REACH:], ROW, shift_pairs(row_count, 1))
    bottom = lax.ppermute(wide[:REACH], ROW, shift_pairs(row_count, -1))
    return jnp.concatenate([top, wide, bottom], axis=0)


def tile_stencil(padded, tap_table, height, breadth):
    summed = jnp.zeros((height, breadth, tap_table.shape[0]), jnp.float32)
    for tap_row in range(KSIZE):
        for tap_col in range(KSIZE):
            window = padded[
                DILATE * tap_row : DILATE * tap_row + height,
                DILATE * tap_col : DILATE * tap_col + breadth,
                :,
            ].astype(jnp.float32)
            summed = summed + tap_table[:, KSIZE * tap_row + tap_col] * window
    return summed


def tile_taps(padded, gradient, height, breadth):
    columns = []
    for tap_row in range(KSIZE):
        for tap_col in range(KSIZE):
            window = padded[
                DILATE * tap_row : DILATE * tap_row + height,
                DILATE * tap_col : DILATE * tap_col + breadth,
                :,
            ].astype(jnp.float32)
            columns.append(jnp.sum(gradient * window, axis=(0, 1)))
    return jnp.stack(columns, axis=1)


def local(image, dw_kernel, ln_gain, w_in, b_in, w_out, layer_scale, cotangent):
    tile_rows, tile_cols, channels = image.shape
    hidden_units = w_in.shape[1]
    row_count = lax.axis_size(ROW)
    col_count = lax.axis_size("col")
    group_count = row_count * col_count
    group_size = channels // group_count
    pixels = tile_rows * tile_cols
    scale_factor = 1.0 / math.sqrt(pixels * group_count)
    full_in, full_out = (
        lax.all_gather(w_in, "col", axis=0, tiled=True),
        lax.all_gather(w_out, "col", axis=0, tiled=True),
    )
    flipped = dw_kernel.reshape(channels, KSIZE, KSIZE)[:, ::-1, ::-1].reshape(
        channels, KSIZE * KSIZE
    )
    padded = add_halo(image)
    conv_tile = tile_stencil(padded, dw_kernel, tile_rows, tile_cols).astype(jnp.bfloat16)
    conv_rows = conv_tile.astype(jnp.float32).reshape(pixels, channels)
    average = jnp.mean(conv_rows, axis=1, keepdims=True)
    centered = conv_rows - average
    inverse = lax.rsqrt(jnp.mean(centered * centered, axis=1, keepdims=True) + EPSILON)
    standard = centered * inverse
    normed = (standard * ln_gain).astype(jnp.bfloat16)
    preact = jnp.dot(normed, full_in, preferred_element_type=jnp.float32) + b_in
    hidden = gelu_exact(preact).astype(jnp.bfloat16)
    mixed = jnp.dot(hidden, full_out, preferred_element_type=jnp.float32)
    out_map = (image.reshape(pixels, channels).astype(jnp.float32) + layer_scale * mixed).astype(
        jnp.bfloat16
    )
    out_map = out_map.reshape(tile_rows, tile_cols, channels)
    upstream = cotangent.reshape(pixels, channels).astype(jnp.float32)
    scale_part = jnp.sum(upstream * mixed, axis=0)
    grad_mix = (upstream * layer_scale).astype(jnp.bfloat16)
    grad_hidden = lax.dot_general(
        grad_mix, full_out, CONTRACT_COLS, preferred_element_type=jnp.float32
    )
    grad_pre = grad_hidden * gelu_slope(preact)
    bias_part = jnp.sum(grad_pre, axis=0)
    grad_pre_rounded = grad_pre.astype(jnp.bfloat16)
    grad_norm = lax.dot_general(
        grad_pre_rounded, full_in, CONTRACT_COLS, preferred_element_type=jnp.float32
    )
    gain_part = jnp.sum(grad_norm * standard, axis=0)
    scaled = grad_norm * ln_gain
    grad_conv = (
        (
            scaled
            - jnp.mean(scaled, axis=1, keepdims=True)
            - standard * jnp.mean(scaled * standard, axis=1, keepdims=True)
        )
        * inverse
    ).astype(jnp.bfloat16)
    grad_conv = grad_conv.reshape(tile_rows, tile_cols, channels)
    grad_padded = add_halo(grad_conv)
    grad_back = tile_stencil(grad_padded, flipped, tile_rows, tile_cols).astype(jnp.bfloat16)
    kernel_part = tile_taps(padded, grad_conv.astype(jnp.float32), tile_rows, tile_cols)
    grad_image = (cotangent.astype(jnp.float32) + grad_back.astype(jnp.float32)).astype(
        jnp.bfloat16
    )
    gain_part = jnp.sum(grad_norm * standard, axis=0)
    rows_out = hidden_units // col_count
    block_in = lax.dot_general(
        normed, grad_pre_rounded, CONTRACT_ROWS, preferred_element_type=jnp.float32
    ).reshape(col_count, rows_out, channels)
    block_out = lax.dot_general(
        hidden, grad_mix, CONTRACT_ROWS, preferred_element_type=jnp.float32
    ).reshape(col_count, rows_out, channels)
    stacked = jnp.stack([block_in, block_out], axis=1)
    halves = lax.psum_scatter(stacked, "core", scatter_dimension=1, tiled=True)
    halves = halves.reshape(-1, channels)
    mine = lax.psum_scatter(halves, "col", scatter_dimension=0, tiled=True)
    mine = lax.psum(mine, "z")
    pair = lax.all_gather(mine, "core", axis=0, tiled=False)
    summed_in = pair[0].reshape(-1, hidden_units)
    summed_out = pair[1]
    small = jnp.concatenate([bias_part, gain_part, scale_part]).reshape(group_count, -1)
    chunk = small.shape[1]
    kernel_cols = group_size * KSIZE * KSIZE
    outgoing = jnp.concatenate(
        [kernel_part.reshape(group_count, kernel_cols), small], axis=1
    )
    incoming = jnp.sum(
        lax.all_to_all(outgoing, EVERY, split_axis=0, concat_axis=0, tiled=True), axis=0
    )
    grad_kernel = incoming[:kernel_cols].reshape(group_size, KSIZE * KSIZE) * scale_factor
    small_mine = incoming[kernel_cols:]
    small_sum = lax.all_to_all(
        jnp.broadcast_to(small_mine[None], (group_count, chunk)),
        EVERY,
        split_axis=0,
        concat_axis=0,
        tiled=True,
    ).reshape(-1)
    bias_sum = small_sum[:hidden_units]
    gain_sum = small_sum[hidden_units : hidden_units + channels]
    scale_sum = small_sum[hidden_units + channels : hidden_units + 2 * channels]
    return (
        out_map,
        grad_image,
        grad_kernel,
        summed_in * scale_factor,
        summed_out * scale_factor,
        bias_sum * scale_factor,
        gain_sum * scale_factor,
        scale_sum * scale_factor,
    )


def solution(mesh):
    devices = mesh.devices.reshape(-1, 2, mesh.devices.shape[1])
    mesh = jax.sharding.Mesh(devices, EVERY)
    tile = P(ROW, "col", None)
    in_specs = (tile, P(), P(), P("col", None), P(), P("col", None), P(), tile)
    out_specs = (tile, tile, P(EVERY, None), P("col", None), P("col", None), P(), P(), P())
    return jax.shard_map(local, mesh=mesh, in_specs=in_specs, out_specs=out_specs, check_vma=False)
```

```python
import math

import jax
import jax.numpy as jnp
from jax import lax
from jax.sharding import PartitionSpec as P

KSIZE = 7
DILATE = 2
REACH = 6


EPSILON = 1e-06
CONTRACT_ROWS = (((0,), (0,)), ((), ()))
CONTRACT_COLS = (((1,), (1,)), ((), ()))


def normal_cdf(values):
    return 0.5 * (1.0 + jax.scipy.special.erf(values * 0.7071067811865476))


def gelu_exact(values):
    return values * normal_cdf(values)


def gelu_slope(values):
    return normal_cdf(values) + values * jnp.exp(-0.5 * values * values) * 0.3989422804014327


def shift_pairs(count, step):
    if step > 0:
        return [(i, i + 1) for i in range(count - 1)]
    return [(i + 1, i) for i in range(count - 1)]


ROW = ("z", "core")
EVERY = ("z", "core", "col")


def add_halo(field):
    row_count = lax.axis_size(ROW)
    col_count = lax.axis_size("col")
    left = lax.ppermute(field[:, -REACH:, :], "col", shift_pairs(col_count, 1))
    right = lax.ppermute(field[:, :REACH, :], "col", shift_pairs(col_count, -1))
    wide = jnp.concatenate([left, field, right], axis=1)
    top = lax.ppermute(wide[-REACH:], ROW, shift_pairs(row_count, 1))
    bottom = lax.ppermute(wide[:REACH], ROW, shift_pairs(row_count, -1))
    return jnp.concatenate([top, wide, bottom], axis=0)


def tile_stencil(padded, tap_table, height, breadth):
    summed = jnp.zeros((height, breadth, tap_table.shape[0]), jnp.float32)
    for tap_row in range(KSIZE):
        for tap_col in range(KSIZE):
            window = padded[
                DILATE * tap_row : DILATE * tap_row + height,
                DILATE * tap_col : DILATE * tap_col + breadth,
                :,
            ].astype(jnp.float32)
            summed = summed + tap_table[:, KSIZE * tap_row + tap_col] * window
    return summed


def tile_taps(padded, gradient, height, breadth):
    columns = []
    for tap_row in range(KSIZE):
        for tap_col in range(KSIZE):
            window = padded[
                DILATE * tap_row : DILATE * tap_row + height,
                DILATE * tap_col : DILATE * tap_col + breadth,
                :,
            ].astype(jnp.float32)
            columns.append(jnp.sum(gradient * window, axis=(0, 1)))
    return jnp.stack(columns, axis=1)


def local(image, dw_kernel, ln_gain, w_in, b_in, w_out, layer_scale, cotangent):
    tile_rows, tile_cols, channels = image.shape
    hidden_units = w_in.shape[1]
    row_count = lax.axis_size(ROW)
    col_count = lax.axis_size("col")
    group_count = row_count * col_count
    group_size = channels // group_count
    pixels = tile_rows * tile_cols
    scale_factor = 1.0 / math.sqrt(pixels * group_count)
    full_in, full_out = (
        lax.all_gather(w_in, "col", axis=0, tiled=True),
        lax.all_gather(w_out, "col", axis=0, tiled=True),
    )
    flipped = dw_kernel.reshape(channels, KSIZE, KSIZE)[:, ::-1, ::-1].reshape(
        channels, KSIZE * KSIZE
    )
    padded = add_halo(image)
    conv_tile = tile_stencil(padded, dw_kernel, tile_rows, tile_cols).astype(jnp.bfloat16)
    conv_rows = conv_tile.astype(jnp.float32).reshape(pixels, channels)
    average = jnp.mean(conv_rows, axis=1, keepdims=True)
    centered = conv_rows - average
    inverse = lax.rsqrt(jnp.mean(centered * centered, axis=1, keepdims=True) + EPSILON)
    standard = centered * inverse
    normed = (standard * ln_gain).astype(jnp.bfloat16)
    preact = jnp.dot(normed, full_in, preferred_element_type=jnp.float32) + b_in
    hidden = gelu_exact(preact).astype(jnp.bfloat16)
    mixed = jnp.dot(hidden, full_out, preferred_element_type=jnp.float32)
    out_map = (image.reshape(pixels, channels).astype(jnp.float32) + layer_scale * mixed).astype(
        jnp.bfloat16
    )
    out_map = out_map.reshape(tile_rows, tile_cols, channels)
    upstream = cotangent.reshape(pixels, channels).astype(jnp.float32)
    scale_part = jnp.sum(upstream * mixed, axis=0)
    grad_mix = (upstream * layer_scale).astype(jnp.bfloat16)
    grad_hidden = lax.dot_general(
        grad_mix, full_out, CONTRACT_COLS, preferred_element_type=jnp.float32
    )
    grad_pre = grad_hidden * gelu_slope(preact)
    bias_part = jnp.sum(grad_pre, axis=0)
    grad_pre_rounded = grad_pre.astype(jnp.bfloat16)
    grad_norm = lax.dot_general(
        grad_pre_rounded, full_in, CONTRACT_COLS, preferred_element_type=jnp.float32
    )
    gain_part = jnp.sum(grad_norm * standard, axis=0)
    scaled = grad_norm * ln_gain
    grad_conv = (
        (
            scaled
            - jnp.mean(scaled, axis=1, keepdims=True)
            - standard * jnp.mean(scaled * standard, axis=1, keepdims=True)
        )
        * inverse
    ).astype(jnp.bfloat16)
    grad_conv = grad_conv.reshape(tile_rows, tile_cols, channels)
    grad_padded = add_halo(grad_conv)
    grad_back = tile_stencil(grad_padded, flipped, tile_rows, tile_cols).astype(jnp.bfloat16)
    kernel_part = tile_taps(padded, grad_conv.astype(jnp.float32), tile_rows, tile_cols)
    grad_image = (cotangent.astype(jnp.float32) + grad_back.astype(jnp.float32)).astype(
        jnp.bfloat16
    )
    gain_part = jnp.sum(grad_norm * standard, axis=0)
    rows_out = hidden_units // col_count
    block_in = lax.dot_general(
        normed, grad_pre_rounded, CONTRACT_ROWS, preferred_element_type=jnp.float32
    ).reshape(col_count, rows_out, channels)
    block_out = lax.dot_general(
        hidden, grad_mix, CONTRACT_ROWS, preferred_element_type=jnp.float32
    ).reshape(col_count, rows_out, channels)
    stacked = jnp.stack([block_in, block_out], axis=1)
    halves = lax.psum_scatter(stacked, "core", scatter_dimension=1, tiled=True)
    halves = halves.reshape(col_count, rows_out, channels)
    mine = jnp.sum(
        lax.all_to_all(halves, "col", split_axis=0, concat_axis=0, tiled=True), axis=0
    )
    mine = lax.psum(mine, "z")
    pair = lax.all_gather(mine, "core", axis=0, tiled=False)
    summed_in = pair[0].reshape(-1, hidden_units)
    summed_out = pair[1]
    small = jnp.concatenate([bias_part, gain_part, scale_part]).reshape(group_count, -1)
    chunk = small.shape[1]
    kernel_cols = group_size * KSIZE * KSIZE
    outgoing = jnp.concatenate(
        [kernel_part.reshape(group_count, kernel_cols), small], axis=1
    )
    incoming = jnp.sum(
        lax.all_to_all(outgoing, EVERY, split_axis=0, concat_axis=0, tiled=True), axis=0
    )
    grad_kernel = incoming[:kernel_cols].reshape(group_size, KSIZE * KSIZE) * scale_factor
    small_mine = incoming[kernel_cols:]
    small_sum = lax.all_to_all(
        jnp.broadcast_to(small_mine[None], (group_count, chunk)),
        EVERY,
        split_axis=0,
        concat_axis=0,
        tiled=True,
    ).reshape(-1)
    bias_sum = small_sum[:hidden_units]
    gain_sum = small_sum[hidden_units : hidden_units + channels]
    scale_sum = small_sum[hidden_units + channels : hidden_units + 2 * channels]
    return (
        out_map,
        grad_image,
        grad_kernel,
        summed_in * scale_factor,
        summed_out * scale_factor,
        bias_sum * scale_factor,
        gain_sum * scale_factor,
        scale_sum * scale_factor,
    )


def solution(mesh):
    devices = mesh.devices.reshape(-1, 2, mesh.devices.shape[1])
    mesh = jax.sharding.Mesh(devices, EVERY)
    tile = P(ROW, "col", None)
    in_specs = (tile, P(), P(), P("col", None), P(), P("col", None), P(), tile)
    out_specs = (tile, tile, P(EVERY, None), P("col", None), P("col", None), P(), P(), P())
    return jax.shard_map(local, mesh=mesh, in_specs=in_specs, out_specs=out_specs, check_vma=False)
```

```python
import math

import jax
import jax.numpy as jnp
from jax import lax
from jax.sharding import PartitionSpec as P

KSIZE = 7
DILATE = 2
REACH = 6


EPSILON = 1e-06
CONTRACT_ROWS = (((0,), (0,)), ((), ()))
CONTRACT_COLS = (((1,), (1,)), ((), ()))


def normal_cdf(values):
    return 0.5 * (1.0 + jax.scipy.special.erf(values * 0.7071067811865476))


def gelu_exact(values):
    return values * normal_cdf(values)


def gelu_slope(values):
    return normal_cdf(values) + values * jnp.exp(-0.5 * values * values) * 0.3989422804014327


def shift_pairs(count, step):
    if step > 0:
        return [(i, i + 1) for i in range(count - 1)]
    return [(i + 1, i) for i in range(count - 1)]


ROW = ("z", "core")
EVERY = ("z", "core", "col")


def add_halo(field):
    row_count = lax.axis_size(ROW)
    col_count = lax.axis_size("col")
    left = lax.ppermute(field[:, -REACH:, :], "col", shift_pairs(col_count, 1))
    right = lax.ppermute(field[:, :REACH, :], "col", shift_pairs(col_count, -1))
    wide = jnp.concatenate([left, field, right], axis=1)
    top = lax.ppermute(wide[-REACH:], ROW, shift_pairs(row_count, 1))
    bottom = lax.ppermute(wide[:REACH], ROW, shift_pairs(row_count, -1))
    return jnp.concatenate([top, wide, bottom], axis=0)


def tile_stencil(padded, tap_table, height, breadth):
    summed = jnp.zeros((height, breadth, tap_table.shape[0]), jnp.float32)
    for tap_row in range(KSIZE):
        for tap_col in range(KSIZE):
            window = padded[
                DILATE * tap_row : DILATE * tap_row + height,
                DILATE * tap_col : DILATE * tap_col + breadth,
                :,
            ].astype(jnp.float32)
            summed = summed + tap_table[:, KSIZE * tap_row + tap_col] * window
    return summed


def tile_taps(padded, gradient, height, breadth):
    columns = []
    for tap_row in range(KSIZE):
        for tap_col in range(KSIZE):
            window = padded[
                DILATE * tap_row : DILATE * tap_row + height,
                DILATE * tap_col : DILATE * tap_col + breadth,
                :,
            ].astype(jnp.float32)
            columns.append(jnp.sum(gradient * window, axis=(0, 1)))
    return jnp.stack(columns, axis=1)


def local(image, dw_kernel, ln_gain, w_in, b_in, w_out, layer_scale, cotangent):
    tile_rows, tile_cols, channels = image.shape
    hidden_units = w_in.shape[1]
    row_count = lax.axis_size(ROW)
    col_count = lax.axis_size("col")
    group_count = row_count * col_count
    group_size = channels // group_count
    pixels = tile_rows * tile_cols
    scale_factor = 1.0 / math.sqrt(pixels * group_count)
    full_in, full_out = (
        lax.all_gather(w_in, "col", axis=0, tiled=True),
        lax.all_gather(w_out, "col", axis=0, tiled=True),
    )
    flipped = dw_kernel.reshape(channels, KSIZE, KSIZE)[:, ::-1, ::-1].reshape(
        channels, KSIZE * KSIZE
    )
    padded = add_halo(image)
    conv_tile = tile_stencil(padded, dw_kernel, tile_rows, tile_cols).astype(jnp.bfloat16)
    conv_rows = conv_tile.astype(jnp.float32).reshape(pixels, channels)
    average = jnp.mean(conv_rows, axis=1, keepdims=True)
    centered = conv_rows - average
    inverse = lax.rsqrt(jnp.mean(centered * centered, axis=1, keepdims=True) + EPSILON)
    standard = centered * inverse
    normed = (standard * ln_gain).astype(jnp.bfloat16)
    preact = jnp.dot(normed, full_in, preferred_element_type=jnp.float32) + b_in
    hidden = gelu_exact(preact).astype(jnp.bfloat16)
    mixed = jnp.dot(hidden, full_out, preferred_element_type=jnp.float32)
    out_map = (image.reshape(pixels, channels).astype(jnp.float32) + layer_scale * mixed).astype(
        jnp.bfloat16
    )
    out_map = out_map.reshape(tile_rows, tile_cols, channels)
    upstream = cotangent.reshape(pixels, channels).astype(jnp.float32)
    scale_part = jnp.sum(upstream * mixed, axis=0)
    grad_mix = (upstream * layer_scale).astype(jnp.bfloat16)
    grad_hidden = lax.dot_general(
        grad_mix, full_out, CONTRACT_COLS, preferred_element_type=jnp.float32
    )
    grad_pre = grad_hidden * gelu_slope(preact)
    bias_part = jnp.sum(grad_pre, axis=0)
    grad_pre_rounded = grad_pre.astype(jnp.bfloat16)
    grad_norm = lax.dot_general(
        grad_pre_rounded, full_in, CONTRACT_COLS, preferred_element_type=jnp.float32
    )
    gain_part = jnp.sum(grad_norm * standard, axis=0)
    scaled = grad_norm * ln_gain
    grad_conv = (
        (
            scaled
            - jnp.mean(scaled, axis=1, keepdims=True)
            - standard * jnp.mean(scaled * standard, axis=1, keepdims=True)
        )
        * inverse
    ).astype(jnp.bfloat16)
    grad_conv = grad_conv.reshape(tile_rows, tile_cols, channels)
    grad_padded = add_halo(grad_conv)
    grad_back = tile_stencil(grad_padded, flipped, tile_rows, tile_cols).astype(jnp.bfloat16)
    kernel_part = tile_taps(padded, grad_conv.astype(jnp.float32), tile_rows, tile_cols)
    grad_image = (cotangent.astype(jnp.float32) + grad_back.astype(jnp.float32)).astype(
        jnp.bfloat16
    )
    gain_part = jnp.sum(grad_norm * standard, axis=0)
    rows_out = hidden_units // col_count
    block_in = lax.dot_general(
        normed, grad_pre_rounded, CONTRACT_ROWS, preferred_element_type=jnp.float32
    ).reshape(col_count, rows_out, channels)
    block_out = lax.dot_general(
        hidden, grad_mix, CONTRACT_ROWS, preferred_element_type=jnp.float32
    ).reshape(col_count, rows_out, channels)
    first_core = lax.axis_index("core") == 0
    sent = jnp.where(first_core, block_out, block_in)
    kept = jnp.where(first_core, block_in, block_out)
    halves = kept + lax.ppermute(sent, "core", [(0, 1), (1, 0)])
    halves = halves.reshape(-1, channels)
    mine = lax.psum_scatter(halves, "col", scatter_dimension=0, tiled=True)
    mine = lax.psum(mine, "z")
    pair = lax.all_gather(mine, "core", axis=0, tiled=False)
    summed_in = pair[0].reshape(-1, hidden_units)
    summed_out = pair[1]
    small = jnp.concatenate([bias_part, gain_part, scale_part]).reshape(group_count, -1)
    chunk = small.shape[1]
    kernel_cols = group_size * KSIZE * KSIZE
    outgoing = jnp.concatenate(
        [kernel_part.reshape(group_count, kernel_cols), small], axis=1
    )
    incoming = jnp.sum(
        lax.all_to_all(outgoing, EVERY, split_axis=0, concat_axis=0, tiled=True), axis=0
    )
    grad_kernel = incoming[:kernel_cols].reshape(group_size, KSIZE * KSIZE) * scale_factor
    small_mine = incoming[kernel_cols:]
    small_sum = lax.all_to_all(
        jnp.broadcast_to(small_mine[None], (group_count, chunk)),
        EVERY,
        split_axis=0,
        concat_axis=0,
        tiled=True,
    ).reshape(-1)
    bias_sum = small_sum[:hidden_units]
    gain_sum = small_sum[hidden_units : hidden_units + channels]
    scale_sum = small_sum[hidden_units + channels : hidden_units + 2 * channels]
    return (
        out_map,
        grad_image,
        grad_kernel,
        summed_in * scale_factor,
        summed_out * scale_factor,
        bias_sum * scale_factor,
        gain_sum * scale_factor,
        scale_sum * scale_factor,
    )


def solution(mesh):
    devices = mesh.devices.reshape(-1, 2, mesh.devices.shape[1])
    mesh = jax.sharding.Mesh(devices, EVERY)
    tile = P(ROW, "col", None)
    in_specs = (tile, P(), P(), P("col", None), P(), P("col", None), P(), tile)
    out_specs = (tile, tile, P(EVERY, None), P("col", None), P("col", None), P(), P(), P())
    return jax.shard_map(local, mesh=mesh, in_specs=in_specs, out_specs=out_specs, check_vma=False)
```

```python
import math

import jax
import jax.numpy as jnp
from jax import lax
from jax.sharding import PartitionSpec as P

KSIZE = 7
DILATE = 2
REACH = 6


EPSILON = 1e-06
CONTRACT_ROWS = (((0,), (0,)), ((), ()))
CONTRACT_COLS = (((1,), (1,)), ((), ()))


def normal_cdf(values):
    return 0.5 * (1.0 + jax.scipy.special.erf(values * 0.7071067811865476))


def gelu_exact(values):
    return values * normal_cdf(values)


def gelu_slope(values):
    return normal_cdf(values) + values * jnp.exp(-0.5 * values * values) * 0.3989422804014327


def shift_pairs(count, step):
    if step > 0:
        return [(i, i + 1) for i in range(count - 1)]
    return [(i + 1, i) for i in range(count - 1)]


ROW = ("z", "core")
EVERY = ("z", "core", "col")


def add_halo(field):
    row_count = lax.axis_size(ROW)
    col_count = lax.axis_size("col")
    left = lax.ppermute(field[:, -REACH:, :], "col", shift_pairs(col_count, 1))
    right = lax.ppermute(field[:, :REACH, :], "col", shift_pairs(col_count, -1))
    wide = jnp.concatenate([left, field, right], axis=1)
    top = lax.ppermute(wide[-REACH:], ROW, shift_pairs(row_count, 1))
    bottom = lax.ppermute(wide[:REACH], ROW, shift_pairs(row_count, -1))
    return jnp.concatenate([top, wide, bottom], axis=0)


def tile_stencil(padded, tap_table, height, breadth):
    summed = jnp.zeros((height, breadth, tap_table.shape[0]), jnp.float32)
    for tap_row in range(KSIZE):
        for tap_col in range(KSIZE):
            window = padded[
                DILATE * tap_row : DILATE * tap_row + height,
                DILATE * tap_col : DILATE * tap_col + breadth,
                :,
            ].astype(jnp.float32)
            summed = summed + tap_table[:, KSIZE * tap_row + tap_col] * window
    return summed


def tile_taps(padded, gradient, height, breadth):
    columns = []
    for tap_row in range(KSIZE):
        for tap_col in range(KSIZE):
            window = padded[
                DILATE * tap_row : DILATE * tap_row + height,
                DILATE * tap_col : DILATE * tap_col + breadth,
                :,
            ].astype(jnp.float32)
            columns.append(jnp.sum(gradient * window, axis=(0, 1)))
    return jnp.stack(columns, axis=1)


def local(image, dw_kernel, ln_gain, w_in, b_in, w_out, layer_scale, cotangent):
    tile_rows, tile_cols, channels = image.shape
    hidden_units = w_in.shape[1]
    row_count = lax.axis_size(ROW)
    col_count = lax.axis_size("col")
    group_count = row_count * col_count
    group_size = channels // group_count
    pixels = tile_rows * tile_cols
    scale_factor = 1.0 / math.sqrt(pixels * group_count)
    full_in, full_out = (
        lax.all_gather(w_in, "col", axis=0, tiled=True),
        lax.all_gather(w_out, "col", axis=0, tiled=True),
    )
    flipped = dw_kernel.reshape(channels, KSIZE, KSIZE)[:, ::-1, ::-1].reshape(
        channels, KSIZE * KSIZE
    )
    padded = add_halo(image)
    conv_tile = tile_stencil(padded, dw_kernel, tile_rows, tile_cols).astype(jnp.bfloat16)
    conv_rows = conv_tile.astype(jnp.float32).reshape(pixels, channels)
    average = jnp.mean(conv_rows, axis=1, keepdims=True)
    centered = conv_rows - average
    inverse = lax.rsqrt(jnp.mean(centered * centered, axis=1, keepdims=True) + EPSILON)
    standard = centered * inverse
    normed = (standard * ln_gain).astype(jnp.bfloat16)
    preact = jnp.dot(normed, full_in, preferred_element_type=jnp.float32) + b_in
    hidden = gelu_exact(preact).astype(jnp.bfloat16)
    mixed = jnp.dot(hidden, full_out, preferred_element_type=jnp.float32)
    out_map = (image.reshape(pixels, channels).astype(jnp.float32) + layer_scale * mixed).astype(
        jnp.bfloat16
    )
    out_map = out_map.reshape(tile_rows, tile_cols, channels)
    upstream = cotangent.reshape(pixels, channels).astype(jnp.float32)
    scale_part = jnp.sum(upstream * mixed, axis=0)
    grad_mix = (upstream * layer_scale).astype(jnp.bfloat16)
    grad_hidden = lax.dot_general(
        grad_mix, full_out, CONTRACT_COLS, preferred_element_type=jnp.float32
    )
    grad_pre = grad_hidden * gelu_slope(preact)
    bias_part = jnp.sum(grad_pre, axis=0)
    grad_pre_rounded = grad_pre.astype(jnp.bfloat16)
    grad_norm = lax.dot_general(
        grad_pre_rounded, full_in, CONTRACT_COLS, preferred_element_type=jnp.float32
    )
    gain_part = jnp.sum(grad_norm * standard, axis=0)
    scaled = grad_norm * ln_gain
    grad_conv = (
        (
            scaled
            - jnp.mean(scaled, axis=1, keepdims=True)
            - standard * jnp.mean(scaled * standard, axis=1, keepdims=True)
        )
        * inverse
    ).astype(jnp.bfloat16)
    grad_conv = grad_conv.reshape(tile_rows, tile_cols, channels)
    grad_padded = add_halo(grad_conv)
    grad_back = tile_stencil(grad_padded, flipped, tile_rows, tile_cols).astype(jnp.bfloat16)
    kernel_part = tile_taps(padded, grad_conv.astype(jnp.float32), tile_rows, tile_cols)
    grad_image = (cotangent.astype(jnp.float32) + grad_back.astype(jnp.float32)).astype(
        jnp.bfloat16
    )
    gain_part = jnp.sum(grad_norm * standard, axis=0)
    rows_out = hidden_units // col_count
    block_in = lax.dot_general(
        normed, grad_pre_rounded, CONTRACT_ROWS, preferred_element_type=jnp.float32
    ).reshape(col_count, rows_out, channels)
    block_out = lax.dot_general(
        hidden, grad_mix, CONTRACT_ROWS, preferred_element_type=jnp.float32
    ).reshape(col_count, rows_out, channels)
    first_core = lax.axis_index("core") == 0
    sent = jnp.where(first_core, block_out, block_in)
    kept = jnp.where(first_core, block_in, block_out)
    halves = kept + lax.ppermute(sent, "core", [(0, 1), (1, 0)])
    halves = halves.reshape(-1, channels)
    mine = lax.psum_scatter(halves, "col", scatter_dimension=0, tiled=True)
    depth = lax.axis_size("z")
    total = mine
    for step in range(1, depth):
        total = total + lax.ppermute(
            mine, "z", [(i, (i + step) % depth) for i in range(depth)]
        )
    other = lax.ppermute(total, "core", [(0, 1), (1, 0)])
    pair = jnp.where(first_core, jnp.stack([total, other]), jnp.stack([other, total]))
    summed_in = pair[0].reshape(-1, hidden_units)
    summed_out = pair[1]
    small = jnp.concatenate([bias_part, gain_part, scale_part]).reshape(group_count, -1)
    chunk = small.shape[1]
    kernel_cols = group_size * KSIZE * KSIZE
    outgoing = jnp.concatenate(
        [kernel_part.reshape(group_count, kernel_cols), small], axis=1
    )
    incoming = jnp.sum(
        lax.all_to_all(outgoing, EVERY, split_axis=0, concat_axis=0, tiled=True), axis=0
    )
    grad_kernel = incoming[:kernel_cols].reshape(group_size, KSIZE * KSIZE) * scale_factor
    small_mine = incoming[kernel_cols:]
    small_sum = lax.all_to_all(
        jnp.broadcast_to(small_mine[None], (group_count, chunk)),
        EVERY,
        split_axis=0,
        concat_axis=0,
        tiled=True,
    ).reshape(-1)
    bias_sum = small_sum[:hidden_units]
    gain_sum = small_sum[hidden_units : hidden_units + channels]
    scale_sum = small_sum[hidden_units + channels : hidden_units + 2 * channels]
    return (
        out_map,
        grad_image,
        grad_kernel,
        summed_in * scale_factor,
        summed_out * scale_factor,
        bias_sum * scale_factor,
        gain_sum * scale_factor,
        scale_sum * scale_factor,
    )


def solution(mesh):
    devices = mesh.devices.reshape(-1, 2, mesh.devices.shape[1])
    mesh = jax.sharding.Mesh(devices, EVERY)
    tile = P(ROW, "col", None)
    in_specs = (tile, P(), P(), P("col", None), P(), P("col", None), P(), tile)
    out_specs = (tile, tile, P(EVERY, None), P("col", None), P("col", None), P(), P(), P())
    return jax.shard_map(local, mesh=mesh, in_specs=in_specs, out_specs=out_specs, check_vma=False)
```

```python
import math

import jax
import jax.numpy as jnp
from jax import lax
from jax.sharding import PartitionSpec as P

KSIZE = 7
DILATE = 2
REACH = 6


EPSILON = 1e-06
CONTRACT_ROWS = (((0,), (0,)), ((), ()))
CONTRACT_COLS = (((1,), (1,)), ((), ()))


def normal_cdf(values):
    return 0.5 * (1.0 + jax.scipy.special.erf(values * 0.7071067811865476))


def gelu_exact(values):
    return values * normal_cdf(values)


def gelu_slope(values):
    return normal_cdf(values) + values * jnp.exp(-0.5 * values * values) * 0.3989422804014327


def shift_pairs(count, step):
    if step > 0:
        return [(i, i + 1) for i in range(count - 1)]
    return [(i + 1, i) for i in range(count - 1)]


ROW = ("z", "core")
EVERY = ("z", "core", "col")


def add_halo(field):
    row_count = lax.axis_size(ROW)
    col_count = lax.axis_size("col")
    left = lax.ppermute(field[:, -REACH:, :], "col", shift_pairs(col_count, 1))
    right = lax.ppermute(field[:, :REACH, :], "col", shift_pairs(col_count, -1))
    wide = jnp.concatenate([left, field, right], axis=1)
    top = lax.ppermute(wide[-REACH:], ROW, shift_pairs(row_count, 1))
    bottom = lax.ppermute(wide[:REACH], ROW, shift_pairs(row_count, -1))
    return jnp.concatenate([top, wide, bottom], axis=0)


def tile_stencil(padded, tap_table, height, breadth):
    summed = jnp.zeros((height, breadth, tap_table.shape[0]), jnp.float32)
    for tap_row in range(KSIZE):
        for tap_col in range(KSIZE):
            window = padded[
                DILATE * tap_row : DILATE * tap_row + height,
                DILATE * tap_col : DILATE * tap_col + breadth,
                :,
            ].astype(jnp.float32)
            summed = summed + tap_table[:, KSIZE * tap_row + tap_col] * window
    return summed


def tile_taps(padded, gradient, height, breadth):
    columns = []
    for tap_row in range(KSIZE):
        for tap_col in range(KSIZE):
            window = padded[
                DILATE * tap_row : DILATE * tap_row + height,
                DILATE * tap_col : DILATE * tap_col + breadth,
                :,
            ].astype(jnp.float32)
            columns.append(jnp.sum(gradient * window, axis=(0, 1)))
    return jnp.stack(columns, axis=1)


def local(image, dw_kernel, ln_gain, w_in, b_in, w_out, layer_scale, cotangent):
    tile_rows, tile_cols, channels = image.shape
    hidden_units = w_in.shape[1]
    row_count = lax.axis_size(ROW)
    col_count = lax.axis_size("col")
    group_count = row_count * col_count
    group_size = channels // group_count
    pixels = tile_rows * tile_cols
    scale_factor = 1.0 / math.sqrt(pixels * group_count)
    full_in, full_out = (
        lax.all_gather(w_in, "col", axis=0, tiled=True),
        lax.all_gather(w_out, "col", axis=0, tiled=True),
    )
    flipped = dw_kernel.reshape(channels, KSIZE, KSIZE)[:, ::-1, ::-1].reshape(
        channels, KSIZE * KSIZE
    )
    padded = add_halo(image)
    conv_tile = tile_stencil(padded, dw_kernel, tile_rows, tile_cols).astype(jnp.bfloat16)
    conv_rows = conv_tile.astype(jnp.float32).reshape(pixels, channels)
    average = jnp.mean(conv_rows, axis=1, keepdims=True)
    centered = conv_rows - average
    inverse = lax.rsqrt(jnp.mean(centered * centered, axis=1, keepdims=True) + EPSILON)
    standard = centered * inverse
    normed = (standard * ln_gain).astype(jnp.bfloat16)
    preact = jnp.dot(normed, full_in, preferred_element_type=jnp.float32) + b_in
    hidden = gelu_exact(preact).astype(jnp.bfloat16)
    mixed = jnp.dot(hidden, full_out, preferred_element_type=jnp.float32)
    out_map = (image.reshape(pixels, channels).astype(jnp.float32) + layer_scale * mixed).astype(
        jnp.bfloat16
    )
    out_map = out_map.reshape(tile_rows, tile_cols, channels)
    upstream = cotangent.reshape(pixels, channels).astype(jnp.float32)
    scale_part = jnp.sum(upstream * mixed, axis=0)
    grad_mix = (upstream * layer_scale).astype(jnp.bfloat16)
    grad_hidden = lax.dot_general(
        grad_mix, full_out, CONTRACT_COLS, preferred_element_type=jnp.float32
    )
    grad_pre = grad_hidden * gelu_slope(preact)
    bias_part = jnp.sum(grad_pre, axis=0)
    grad_pre_rounded = grad_pre.astype(jnp.bfloat16)
    grad_norm = lax.dot_general(
        grad_pre_rounded, full_in, CONTRACT_COLS, preferred_element_type=jnp.float32
    )
    gain_part = jnp.sum(grad_norm * standard, axis=0)
    scaled = grad_norm * ln_gain
    grad_conv = (
        (
            scaled
            - jnp.mean(scaled, axis=1, keepdims=True)
            - standard * jnp.mean(scaled * standard, axis=1, keepdims=True)
        )
        * inverse
    ).astype(jnp.bfloat16)
    grad_conv = grad_conv.reshape(tile_rows, tile_cols, channels)
    grad_padded = add_halo(grad_conv)
    grad_back = tile_stencil(grad_padded, flipped, tile_rows, tile_cols).astype(jnp.bfloat16)
    kernel_part = tile_taps(padded, grad_conv.astype(jnp.float32), tile_rows, tile_cols)
    grad_image = (cotangent.astype(jnp.float32) + grad_back.astype(jnp.float32)).astype(
        jnp.bfloat16
    )
    gain_part = jnp.sum(grad_norm * standard, axis=0)
    rows_out = hidden_units // col_count
    block_in = lax.dot_general(
        normed, grad_pre_rounded, CONTRACT_ROWS, preferred_element_type=jnp.float32
    ).reshape(col_count, rows_out, channels)
    block_out = lax.dot_general(
        hidden, grad_mix, CONTRACT_ROWS, preferred_element_type=jnp.float32
    ).reshape(col_count, rows_out, channels)
    first_core = lax.axis_index("core") == 0
    sent = jnp.where(first_core, block_out, block_in)
    kept = jnp.where(first_core, block_in, block_out)
    halves = kept + lax.ppermute(sent, "core", [(0, 1), (1, 0)])
    halves = halves.reshape(-1, channels)
    mine = lax.psum_scatter(halves, "col", scatter_dimension=0, tiled=True)
    grad_image, mine = lax.optimization_barrier((grad_image, mine))
    depth = lax.axis_size("z")
    total = mine
    for step in range(1, depth):
        total = total + lax.ppermute(
            mine, "z", [(i, (i + step) % depth) for i in range(depth)]
        )
    other = lax.ppermute(total, "core", [(0, 1), (1, 0)])
    pair = jnp.where(first_core, jnp.stack([total, other]), jnp.stack([other, total]))
    summed_in = pair[0].reshape(-1, hidden_units)
    summed_out = pair[1]
    small = jnp.concatenate([bias_part, gain_part, scale_part]).reshape(group_count, -1)
    chunk = small.shape[1]
    kernel_cols = group_size * KSIZE * KSIZE
    outgoing = jnp.concatenate(
        [kernel_part.reshape(group_count, kernel_cols), small], axis=1
    )
    incoming = jnp.sum(
        lax.all_to_all(outgoing, EVERY, split_axis=0, concat_axis=0, tiled=True), axis=0
    )
    grad_kernel = incoming[:kernel_cols].reshape(group_size, KSIZE * KSIZE) * scale_factor
    small_mine = incoming[kernel_cols:]
    small_sum = lax.all_to_all(
        jnp.broadcast_to(small_mine[None], (group_count, chunk)),
        EVERY,
        split_axis=0,
        concat_axis=0,
        tiled=True,
    ).reshape(-1)
    bias_sum = small_sum[:hidden_units]
    gain_sum = small_sum[hidden_units : hidden_units + channels]
    scale_sum = small_sum[hidden_units + channels : hidden_units + 2 * channels]
    return (
        out_map,
        grad_image,
        grad_kernel,
        summed_in * scale_factor,
        summed_out * scale_factor,
        bias_sum * scale_factor,
        gain_sum * scale_factor,
        scale_sum * scale_factor,
    )


def solution(mesh):
    devices = mesh.devices.reshape(-1, 2, mesh.devices.shape[1])
    mesh = jax.sharding.Mesh(devices, EVERY)
    tile = P(ROW, "col", None)
    in_specs = (tile, P(), P(), P("col", None), P(), P("col", None), P(), tile)
    out_specs = (tile, tile, P(EVERY, None), P("col", None), P("col", None), P(), P(), P())
    return jax.shard_map(local, mesh=mesh, in_specs=in_specs, out_specs=out_specs, check_vma=False)
```
